256 devices in a mesh: ctx: 8 (over x, y_lo), chan: 32 (over z, y_hi, core).
Axes of the slice: x: 4, y: 4 (y_hi: 2, y_lo: 2; y = y_hi * 2 + y_lo), z: 8, core: 2. Of those that a mesh axis runs over, the one named last changes fastest.
Arguments:
- gate_input: bfloat16 [1024, 8192], P('ctx', 'chan'), may hold values from -6 to 6
- key_input: bfloat16 [1024, 8192], P('ctx', 'chan'), may hold values from -6 to 6
- value_input: bfloat16 [1024, 8192], P('ctx', 'chan'), may hold values from -6 to 6
- short_filters: float32 [3, 7, 8192], P(None, None, 'chan'), may hold values from -2.5 to 2.5
- pole_time: float32 [8192, 16], P('chan'), may hold values from 30 to 2048
- residues: float32 [8192, 16], P('chan'), may hold values from -1.5 to 1.5
- out_weight: bfloat16 [8192, 8192], P('ctx', 'chan'), may hold values from -0.125 to 0.125
- out_cotangent: bfloat16 [1024, 8192], P('ctx', 'chan'), may hold values from -6 to 6
Outputs:
- block_output: bfloat16 [1024, 8192], P('ctx', 'chan')
- gate_grad: bfloat16 [1024, 8192], P('ctx', 'chan')
- key_grad: bfloat16 [1024, 8192], P('ctx', 'chan')
- value_grad: bfloat16 [1024, 8192], P('ctx', 'chan')
The draws below stay inside these ranges and needn't reach their ends.
All inputs are finite; a program needn't handle non-finite values.
Results may differ from the reference program's by a relative error of at most 0.0049.
Values may be sent and summed in bfloat16 or wider, within the bound.
No kernel may reach another device: no remote copies, remote signals or barrier semaphores. Data moves between devices by JAX's collectives and lax.ppermute only.
A program may use at most 64 MiB of HBM per device.

```python
import math
import jax
import jax.numpy as jnp
from jax import lax

D = 8192
M = 16
TAPS = 7
SEQ = 1024


def raised(values, key, source, target, shards_of, factor):
    owner, partner = [(jnp.arange(values.shape[dim]) // (values.shape[dim] // shards_of)).reshape([-1 if axis == dim else 1 for axis in range(values.ndim)]) for dim in (source, target)]
    chosen = jax.random.permutation(key, shards_of)[partner]
    strong = (owner == chosen) | (owner == (partner + shards_of // 2) % shards_of)
    return jnp.where(strong, factor * values, values)


def level_of(rng, extent, split, smallest, high):
    gain, own = 1.0, jax.random.fold_in(rng, 6)
    for position, shards_of in split:
        heights = jnp.exp(jax.random.uniform(jax.random.fold_in(own, position), (shards_of,), jnp.float32, smallest / len(split), high / len(split)))
        gain = gain * jnp.repeat(heights, extent[position] // shards_of).reshape([-1 if axis == position else 1 for axis in range(len(extent))])
    return gain


def bell_draw(rng, dims, width, reach, pieces=(), kind=jnp.bfloat16):
    array = width * jax.random.normal(rng, dims, jnp.float32)
    if pieces:
        array = array * level_of(rng, dims, pieces, -0.22, 0.18)
    return jnp.clip(array, -reach, reach).astype(kind)


def bell_draw_with(rng, dims, deviation, reach, shards, heavy, kind=jnp.bfloat16):
    drawn = deviation * jax.random.normal(rng, dims, jnp.float32)
    if shards:
        drawn = drawn * level_of(rng, dims, shards, -0.22, 0.18)
    return jnp.clip(raised(drawn, jax.random.fold_in(rng, 3), *heavy), -reach, reach).astype(kind)


def setup_inputs(seed: int = 0) -> dict:
    key_of = jax.random.split(jax.random.key(seed), 9)
    gate_input = bell_draw(key_of[0], (SEQ, D), 1.0, 6.0, ((0, 8), (1, 32)))
    key_input = bell_draw(key_of[1], (SEQ, D), 1.0, 6.0, ((0, 8), (1, 32)))
    value_input = bell_draw(key_of[2], (SEQ, D), 1.0, 6.0, ((0, 8), (1, 32)))
    short_filters = bell_draw(key_of[3], (3, TAPS, D), 0.4, 2.5, ((2, 32),), jnp.float32)
    pole_time = jnp.clip(jnp.exp(math.log(2048.0) - 4.2234216 * jax.random.uniform(key_of[4], (D, M), jnp.float32) ** level_of(key_of[4], (D, M), ((0, 32),), -0.2, 0.2)), 30.0, 2048.0)
    residues = bell_draw(key_of[5], (D, M), 0.25, 1.5, ((0, 32),), jnp.float32)
    out_weight = bell_draw_with(key_of[6], (D, D), D ** -0.5, 0.125, ((0, 8), (1, 32)), (1, 0, 32, 2.75))
    out_cotangent = bell_draw(key_of[7], (SEQ, D), 1.0, 6.0, ((0, 8), (1, 32)))
    return dict(gate_input=gate_input, key_input=key_input, value_input=value_input, short_filters=short_filters, pole_time=pole_time, residues=residues, out_weight=out_weight, out_cotangent=out_cotangent)


def causal_taps(signal, filter_taps):
    tap_count = filter_taps.shape[0]
    length = signal.shape[0]
    padded = jnp.pad(signal, ((tap_count - 1, 0), (0, 0)))
    summed = jnp.zeros_like(signal)
    for offset in range(tap_count):
        lead_row = tap_count - 1 - offset
        summed = summed + filter_taps[offset][None, :] * padded[lead_row:lead_row + length]
    return summed

def anti_taps(signal, filter_taps):
    tap_count = filter_taps.shape[0]
    length = signal.shape[0]
    padded = jnp.pad(signal, ((0, tap_count - 1), (0, 0)))
    summed = jnp.zeros_like(signal)
    for offset in range(tap_count):
        summed = summed + filter_taps[offset][None, :] * padded[offset:offset + length]
    return summed

def modal_scan(signal, decay, modal_weight, backward):

    def advance(state, row_values):
        state = decay * state + row_values[None, :]
        return (state, lax.optimization_barrier(jnp.sum(modal_weight * state, axis=0)))
    start_state = jnp.zeros(decay.shape, decay.dtype)
    _, result = lax.scan(advance, start_state, signal, reverse=backward)
    return result

def reference(gate_input, key_input, value_input, short_filters, pole_time, residues, out_weight, out_cotangent):
    gate_short = causal_taps(gate_input.astype(jnp.float32), short_filters[0])
    key_short = causal_taps(key_input.astype(jnp.float32), short_filters[1])
    value_short = causal_taps(value_input.astype(jnp.float32), short_filters[2])
    mixed = key_short * value_short
    inv_time = 1.0 / pole_time.T
    modal_weight = residues.T * jnp.sqrt(-jnp.expm1(-2.0 * inv_time))
    decay = jnp.exp(-inv_time)
    long_out = modal_scan(mixed, decay, modal_weight, False)
    gated = (gate_short * long_out).astype(jnp.bfloat16)
    block_output = jnp.dot(gated, out_weight, preferred_element_type=jnp.float32).astype(jnp.bfloat16)
    grad_gated = lax.dot_general(out_cotangent, out_weight, (((1,), (1,)), ((), ())), preferred_element_type=jnp.float32)
    grad_gate_short = grad_gated * long_out
    grad_long = grad_gated * gate_short
    grad_mixed = modal_scan(grad_long, decay, modal_weight, True)
    grad_key_short = grad_mixed * value_short
    grad_value_short = grad_mixed * key_short
    gate_grad = anti_taps(grad_gate_short, short_filters[0]).astype(jnp.bfloat16)
    key_grad = anti_taps(grad_key_short, short_filters[1]).astype(jnp.bfloat16)
    value_grad = anti_taps(grad_value_short, short_filters[2]).astype(jnp.bfloat16)
    return (block_output, gate_grad, key_grad, value_grad)
```

```python
import math

import jax
import jax.numpy as jnp
from jax import lax
from jax.sharding import PartitionSpec as P

HIGHEST = lax.Precision.HIGHEST


def from_behind(block, axis, distance):
    devices = range(lax.axis_size(axis))
    route = [(i - distance, i) for i in devices if i - distance in devices]
    return lax.ppermute(block, axis, route)


def gather_ctx(block):
    peers, position = (lax.axis_size("ctx"), lax.axis_index("ctx"))
    recv = [block] + [
        lax.ppermute(block, "ctx", [(i, (i + d) % peers) for i in range(peers)])
        for d in range(1, peers)
    ]
    full = jnp.zeros((peers,) + block.shape, block.dtype)
    for d in range(peers):
        full = lax.dynamic_update_index_in_dim(full, recv[d], (position - d) % peers, 0)
    return full


def carried_in(every, block_decay, reverse):
    peers, position = (every.shape[0], lax.axis_index("ctx"))
    state = jnp.zeros_like(block_decay)
    for at in range(peers - 1, -1, -1) if reverse else range(peers):
        reached = at > position if reverse else at < position
        state = jnp.where(reached, block_decay * state + every[at], state)
    return state


def causal_taps(extended, filter_taps, length):
    tap_count = filter_taps.shape[0]
    summed = jnp.zeros((length, extended.shape[1]), jnp.float32)
    for offset in range(tap_count):
        lead_row = tap_count - 1 - offset
        summed = summed + filter_taps[offset][None, :] * extended[lead_row : lead_row + length]
    return summed


def anti_taps(extended, filter_taps, length):
    tap_count = filter_taps.shape[0]
    summed = jnp.zeros((length, extended.shape[1]), jnp.float32)
    for offset in range(tap_count):
        summed = summed + filter_taps[offset][None, :] * extended[offset : offset + length]
    return summed


def spectral_tables(length):
    doubled = 2 * length
    freqs = lax.broadcasted_iota(jnp.int32, (doubled, length), 0)
    places = lax.broadcasted_iota(jnp.int32, (doubled, length), 1)
    angles = (freqs * places % doubled).astype(jnp.float32) * (2.0 * math.pi / doubled)
    forward = jnp.concatenate([jnp.cos(angles), -jnp.sin(angles)], axis=0)
    inverse = forward.T / doubled
    return (forward, inverse)


def apply_filter(spectrum, signal, forward, inverse):
    middle = forward.shape[0] // 2
    spectra = jnp.dot(forward, signal, precision=HIGHEST)
    real_sig = spectra[:middle]
    imag_sig = spectra[middle:]
    real_filt = spectrum[:middle]
    imag_filt = spectrum[middle:]
    product = jnp.concatenate(
        [real_sig * real_filt - imag_sig * imag_filt, real_sig * imag_filt + imag_sig * real_filt],
        axis=0,
    )
    return jnp.dot(inverse, product, precision=HIGHEST)


def mode_sums(inv_time, modal_weight, mixed, length):
    offsets = lax.broadcasted_iota(jnp.float32, (length, 1), 0)

    def one_mode(carry, pieces):
        rate_row, weight_row = pieces
        decay = jnp.exp(-offsets * rate_row[None, :])
        forward_sum = jnp.sum(decay[::-1] * mixed, axis=0)
        return (carry + weight_row[None, :] * decay, forward_sum)

    start_filter = jnp.zeros((length, mixed.shape[1]), jnp.float32)
    return lax.scan(one_mode, start_filter, (inv_time, modal_weight))


def mode_sums_back(inv_time, grad_long, length):
    offsets = lax.broadcasted_iota(jnp.float32, (length, 1), 0)

    def one_mode(carry, rate_row):
        decay = jnp.exp(-offsets * rate_row[None, :])
        return (carry, jnp.sum(decay * grad_long, axis=0))

    return lax.scan(one_mode, 0, inv_time)[1]


def mode_terms(inv_time, modal_weight, state, length, backward):
    offsets = lax.broadcasted_iota(jnp.float32, (length, 1), 0)

    def one_mode(carry, pieces):
        rate_row, weight_row, state_row = pieces
        decay = jnp.exp(-offsets * rate_row[None, :])
        step_decay = (weight_row * jnp.exp(-rate_row))[None, :]
        term = step_decay * (decay[::-1] if backward else decay) * state_row[None, :]
        return (carry + term, None)

    start_terms = jnp.zeros((length, inv_time.shape[1]), jnp.float32)
    return lax.scan(one_mode, start_terms, (inv_time, modal_weight, state))[0]


def body(
    gate_input,
    key_input,
    value_input,
    short_filters,
    pole_time,
    residues,
    out_weight,
    out_cotangent,
):
    length = gate_input.shape[0]
    tap_count = short_filters.shape[1]
    weight_full = gather_ctx(out_weight).reshape(-1, out_weight.shape[1])
    stacked = jnp.stack([gate_input, key_input, value_input])
    tails = from_behind(stacked[:, length - (tap_count - 1) :, :], "ctx", 1)
    extended = jnp.concatenate([tails, stacked], axis=1).astype(jnp.float32)
    gate_short = causal_taps(extended[0], short_filters[0], length)
    key_short = causal_taps(extended[1], short_filters[1], length)
    value_short = causal_taps(extended[2], short_filters[2], length)
    mixed = key_short * value_short
    inv_time = 1.0 / pole_time.T
    modal_weight = residues.T * jnp.sqrt(-jnp.expm1(-2.0 * inv_time))
    block_decay = jnp.exp(-float(length) * inv_time)
    filt_table, forward_sums = mode_sums(inv_time, modal_weight, mixed, length)
    state_in = carried_in(gather_ctx(forward_sums), block_decay, False)
    forward, inverse = spectral_tables(length)
    spectrum = jnp.dot(forward, filt_table, precision=HIGHEST)
    long_local = apply_filter(spectrum, mixed, forward, inverse)
    long_out = long_local + mode_terms(inv_time, modal_weight, state_in, length, False)
    gated = (gate_short * long_out).astype(jnp.bfloat16)
    gated_full = lax.all_gather(gated, "chan", axis=1, tiled=True)
    partial = lax.dot_general(
        weight_full, out_cotangent, (((1,), (1,)), ((), ())), preferred_element_type=jnp.float32
    )
    peers = lax.axis_size("chan")
    partial, _ = lax.optimization_barrier((partial, gated))
    arrived = lax.all_to_all(partial, "chan", 0, 0, tiled=True)
    grad_gated = jnp.sum(arrived.reshape(peers, -1, arrived.shape[1]), axis=0).T
    grad_long = grad_gated * gate_short
    backward_sums = mode_sums_back(inv_time, grad_long, length)
    state_back = carried_in(gather_ctx(backward_sums), block_decay, True)
    back_local = apply_filter(spectrum, grad_long[::-1], forward, inverse)[::-1]
    grad_mixed = back_local + mode_terms(inv_time, modal_weight, state_back, length, True)
    block_output = jnp.dot(gated_full, weight_full, preferred_element_type=jnp.float32).astype(
        jnp.bfloat16
    )
    grad_gate_short = grad_gated * long_out
    grad_key_short = grad_mixed * value_short
    grad_value_short = grad_mixed * key_short
    grads = jnp.stack([grad_gate_short, grad_key_short, grad_value_short])
    heads = from_behind(grads[:, : tap_count - 1, :], "ctx", -1)
    ext_grads = jnp.concatenate([grads, heads], axis=1)
    gate_grad = anti_taps(ext_grads[0], short_filters[0], length).astype(jnp.bfloat16)
    key_grad = anti_taps(ext_grads[1], short_filters[1], length).astype(jnp.bfloat16)
    value_grad = anti_taps(ext_grads[2], short_filters[2], length).astype(jnp.bfloat16)
    return (block_output, gate_grad, key_grad, value_grad)


def solution(mesh):
    in_specs = (
        P("ctx", "chan"),
        P("ctx", "chan"),
        P("ctx", "chan"),
        P(None, None, "chan"),
        P("chan", None),
        P("chan", None),
        P("ctx", "chan"),
        P("ctx", "chan"),
    )
    out_specs = (P("ctx", "chan"), P("ctx", "chan"), P("ctx", "chan"), P("ctx", "chan"))
    return jax.shard_map(body, mesh=mesh, in_specs=in_specs, out_specs=out_specs, check_vma=False)
```

```python
import math

import jax
import jax.numpy as jnp
from jax import lax
from jax.sharding import PartitionSpec as P

HIGHEST = lax.Precision.HIGHEST


def from_behind(block, axis, distance):
    devices = range(lax.axis_size(axis))
    route = [(i - distance, i) for i in devices if i - distance in devices]
    return lax.ppermute(block, axis, route)


def gather_ctx(block):
    peers, position = (lax.axis_size("ctx"), lax.axis_index("ctx"))
    recv = [block] + [
        lax.ppermute(block, "ctx", [(i, (i + d) % peers) for i in range(peers)])
        for d in range(1, peers)
    ]
    full = jnp.zeros((peers,) + block.shape, block.dtype)
    for d in range(peers):
        full = lax.dynamic_update_index_in_dim(full, recv[d], (position - d) % peers, 0)
    return full


def reduce_chan(partial):
    peers, position = (lax.axis_size("chan"), lax.axis_index("chan"))
    chunks = partial.reshape(peers // 2, 2, -1, partial.shape[1])
    keep = lax.dynamic_index_in_dim(chunks, position % 2, axis=1, keepdims=False)
    give = lax.dynamic_index_in_dim(chunks, 1 - position % 2, axis=1, keepdims=False)
    half = keep + lax.ppermute(give, "chan", [(j, j ^ 1) for j in range(peers)])
    groups = [list(range(b, peers, 2)) for b in range(2)]
    arrived = lax.all_to_all(half, "chan", 0, 0, axis_index_groups=groups, tiled=True)
    return jnp.sum(arrived, axis=0)


def carried_in(every, block_decay, reverse):
    peers, position = (every.shape[0], lax.axis_index("ctx"))
    state = jnp.zeros_like(block_decay)
    for at in range(peers - 1, -1, -1) if reverse else range(peers):
        reached = at > position if reverse else at < position
        state = jnp.where(reached, block_decay * state + every[at], state)
    return state


def causal_taps(extended, filter_taps, length):
    tap_count = filter_taps.shape[0]
    summed = jnp.zeros((length, extended.shape[1]), jnp.float32)
    for offset in range(tap_count):
        lead_row = tap_count - 1 - offset
        summed = summed + filter_taps[offset][None, :] * extended[lead_row : lead_row + length]
    return summed


def anti_taps(extended, filter_taps, length):
    tap_count = filter_taps.shape[0]
    summed = jnp.zeros((length, extended.shape[1]), jnp.float32)
    for offset in range(tap_count):
        summed = summed + filter_taps[offset][None, :] * extended[offset : offset + length]
    return summed


def spectral_tables(length):
    doubled = 2 * length
    freqs = lax.broadcasted_iota(jnp.int32, (doubled, length), 0)
    places = lax.broadcasted_iota(jnp.int32, (doubled, length), 1)
    angles = (freqs * places % doubled).astype(jnp.float32) * (2.0 * math.pi / doubled)
    forward = jnp.concatenate([jnp.cos(angles), -jnp.sin(angles)], axis=0)
    inverse = forward.T / doubled
    return (forward, inverse)


def apply_filter(spectrum, signal, forward, inverse):
    middle = forward.shape[0] // 2
    spectra = jnp.dot(forward, signal, precision=HIGHEST)
    real_sig = spectra[:middle]
    imag_sig = spectra[middle:]
    real_filt = spectrum[:middle]
    imag_filt = spectrum[middle:]
    product = jnp.concatenate(
        [real_sig * real_filt - imag_sig * imag_filt, real_sig * imag_filt + imag_sig * real_filt],
        axis=0,
    )
    return jnp.dot(inverse, product, precision=HIGHEST)


def mode_sums(inv_time, modal_weight, mixed, length):
    offsets = lax.broadcasted_iota(jnp.float32, (length, 1), 0)

    def one_mode(carry, pieces):
        rate_row, weight_row = pieces
        decay = jnp.exp(-offsets * rate_row[None, :])
        forward_sum = jnp.sum(decay[::-1] * mixed, axis=0)
        return (carry + weight_row[None, :] * decay, forward_sum)

    start_filter = jnp.zeros((length, mixed.shape[1]), jnp.float32)
    return lax.scan(one_mode, start_filter, (inv_time, modal_weight))


def mode_sums_back(inv_time, grad_long, length):
    offsets = lax.broadcasted_iota(jnp.float32, (length, 1), 0)

    def one_mode(carry, rate_row):
        decay = jnp.exp(-offsets * rate_row[None, :])
        return (carry, jnp.sum(decay * grad_long, axis=0))

    return lax.scan(one_mode, 0, inv_time)[1]


def mode_terms(inv_time, modal_weight, state, length, backward):
    offsets = lax.broadcasted_iota(jnp.float32, (length, 1), 0)

    def one_mode(carry, pieces):
        rate_row, weight_row, state_row = pieces
        decay = jnp.exp(-offsets * rate_row[None, :])
        step_decay = (weight_row * jnp.exp(-rate_row))[None, :]
        term = step_decay * (decay[::-1] if backward else decay) * state_row[None, :]
        return (carry + term, None)

    start_terms = jnp.zeros((length, inv_time.shape[1]), jnp.float32)
    return lax.scan(one_mode, start_terms, (inv_time, modal_weight, state))[0]


def body(
    gate_input,
    key_input,
    value_input,
    short_filters,
    pole_time,
    residues,
    out_weight,
    out_cotangent,
):
    length = gate_input.shape[0]
    tap_count = short_filters.shape[1]
    weight_full = gather_ctx(out_weight).reshape(-1, out_weight.shape[1])
    stacked = jnp.stack([gate_input, key_input, value_input])
    tails = from_behind(stacked[:, length - (tap_count - 1) :, :], "ctx", 1)
    extended = jnp.concatenate([tails, stacked], axis=1).astype(jnp.float32)
    gate_short = causal_taps(extended[0], short_filters[0], length)
    key_short = causal_taps(extended[1], short_filters[1], length)
    value_short = causal_taps(extended[2], short_filters[2], length)
    mixed = key_short * value_short
    inv_time = 1.0 / pole_time.T
    modal_weight = residues.T * jnp.sqrt(-jnp.expm1(-2.0 * inv_time))
    block_decay = jnp.exp(-float(length) * inv_time)
    filt_table, forward_sums = mode_sums(inv_time, modal_weight, mixed, length)
    state_in = carried_in(gather_ctx(forward_sums), block_decay, False)
    forward, inverse = spectral_tables(length)
    spectrum = jnp.dot(forward, filt_table, precision=HIGHEST)
    long_local = apply_filter(spectrum, mixed, forward, inverse)
    long_out = long_local + mode_terms(inv_time, modal_weight, state_in, length, False)
    gated = (gate_short * long_out).astype(jnp.bfloat16)
    gated_full = lax.all_gather(gated, "chan", axis=1, tiled=True)
    partial = lax.dot_general(
        weight_full, out_cotangent, (((1,), (1,)), ((), ())), preferred_element_type=jnp.float32
    )
    partial, _ = lax.optimization_barrier((partial, gated))
    grad_gated = reduce_chan(partial).T
    grad_long = grad_gated * gate_short
    backward_sums = mode_sums_back(inv_time, grad_long, length)
    state_back = carried_in(gather_ctx(backward_sums), block_decay, True)
    back_local = apply_filter(spectrum, grad_long[::-1], forward, inverse)[::-1]
    grad_mixed = back_local + mode_terms(inv_time, modal_weight, state_back, length, True)
    block_output = jnp.dot(gated_full, weight_full, preferred_element_type=jnp.float32).astype(
        jnp.bfloat16
    )
    grad_gate_short = grad_gated * long_out
    grad_key_short = grad_mixed * value_short
    grad_value_short = grad_mixed * key_short
    grads = jnp.stack([grad_gate_short, grad_key_short, grad_value_short])
    heads = from_behind(grads[:, : tap_count - 1, :], "ctx", -1)
    ext_grads = jnp.concatenate([grads, heads], axis=1)
    gate_grad = anti_taps(ext_grads[0], short_filters[0], length).astype(jnp.bfloat16)
    key_grad = anti_taps(ext_grads[1], short_filters[1], length).astype(jnp.bfloat16)
    value_grad = anti_taps(ext_grads[2], short_filters[2], length).astype(jnp.bfloat16)
    return (block_output, gate_grad, key_grad, value_grad)


def solution(mesh):
    in_specs = (
        P("ctx", "chan"),
        P("ctx", "chan"),
        P("ctx", "chan"),
        P(None, None, "chan"),
        P("chan", None),
        P("chan", None),
        P("ctx", "chan"),
        P("ctx", "chan"),
    )
    out_specs = (P("ctx", "chan"), P("ctx", "chan"), P("ctx", "chan"), P("ctx", "chan"))
    return jax.shard_map(body, mesh=mesh, in_specs=in_specs, out_specs=out_specs, check_vma=False)
```

```python
import math

import jax
import jax.numpy as jnp
from jax import lax
from jax.sharding import PartitionSpec as P

HIGHEST = lax.Precision.HIGHEST


def from_behind(block, axis, distance):
    devices = range(lax.axis_size(axis))
    route = [(i - distance, i) for i in devices if i - distance in devices]
    return lax.ppermute(block, axis, route)


def gather_ctx(block):
    peers, position = (lax.axis_size("ctx"), lax.axis_index("ctx"))
    recv = [block] + [
        lax.ppermute(block, "ctx", [(i, (i + d) % peers) for i in range(peers)])
        for d in range(1, peers)
    ]
    order = (position - jnp.arange(peers)) % peers
    return jnp.take(jnp.stack(recv), order, axis=0)


def reduce_chan(partial):
    peers, position = (lax.axis_size("chan"), lax.axis_index("chan"))
    chunks = partial.reshape(peers // 2, 2, -1, partial.shape[1])
    keep = lax.dynamic_index_in_dim(chunks, position % 2, axis=1, keepdims=False)
    give = lax.dynamic_index_in_dim(chunks, 1 - position % 2, axis=1, keepdims=False)
    half = keep + lax.ppermute(give, "chan", [(j, j ^ 1) for j in range(peers)])
    groups = [list(range(b, peers, 2)) for b in range(2)]
    arrived = lax.all_to_all(half, "chan", 0, 0, axis_index_groups=groups, tiled=True)
    return jnp.sum(arrived, axis=0)


def carried_in(every, block_decay, reverse):
    peers, position = (every.shape[0], lax.axis_index("ctx"))
    state = jnp.zeros_like(block_decay)
    for at in range(peers - 1, -1, -1) if reverse else range(peers):
        reached = at > position if reverse else at < position
        state = jnp.where(reached, block_decay * state + every[at], state)
    return state


def causal_taps(extended, filter_taps, length):
    tap_count = filter_taps.shape[0]
    summed = jnp.zeros((length, extended.shape[1]), jnp.float32)
    for offset in range(tap_count):
        lead_row = tap_count - 1 - offset
        summed = summed + filter_taps[offset][None, :] * extended[lead_row : lead_row + length]
    return summed


def anti_taps(extended, filter_taps, length):
    tap_count = filter_taps.shape[0]
    summed = jnp.zeros((length, extended.shape[1]), jnp.float32)
    for offset in range(tap_count):
        summed = summed + filter_taps[offset][None, :] * extended[offset : offset + length]
    return summed


def spectral_tables(length):
    doubled = 2 * length
    freqs = lax.broadcasted_iota(jnp.int32, (doubled, length), 0)
    places = lax.broadcasted_iota(jnp.int32, (doubled, length), 1)
    angles = (freqs * places % doubled).astype(jnp.float32) * (2.0 * math.pi / doubled)
    forward = jnp.concatenate([jnp.cos(angles), -jnp.sin(angles)], axis=0)
    inverse = forward.T / doubled
    return (forward, inverse)


def apply_filter(spectrum, signal, forward, inverse):
    middle = forward.shape[0] // 2
    spectra = jnp.dot(forward, signal, precision=HIGHEST)
    real_sig = spectra[:middle]
    imag_sig = spectra[middle:]
    real_filt = spectrum[:middle]
    imag_filt = spectrum[middle:]
    product = jnp.concatenate(
        [real_sig * real_filt - imag_sig * imag_filt, real_sig * imag_filt + imag_sig * real_filt],
        axis=0,
    )
    return jnp.dot(inverse, product, precision=HIGHEST)


def mode_sums(inv_time, modal_weight, mixed, length):
    offsets = lax.broadcasted_iota(jnp.float32, (length, 1), 0)

    def one_mode(carry, pieces):
        rate_row, weight_row = pieces
        decay = jnp.exp(-offsets * rate_row[None, :])
        forward_sum = jnp.sum(decay[::-1] * mixed, axis=0)
        return (carry + weight_row[None, :] * decay, forward_sum)

    start_filter = jnp.zeros((length, mixed.shape[1]), jnp.float32)
    return lax.scan(one_mode, start_filter, (inv_time, modal_weight))


def mode_sums_back(inv_time, grad_long, length):
    offsets = lax.broadcasted_iota(jnp.float32, (length, 1), 0)

    def one_mode(carry, rate_row):
        decay = jnp.exp(-offsets * rate_row[None, :])
        return (carry, jnp.sum(decay * grad_long, axis=0))

    return lax.scan(one_mode, 0, inv_time)[1]


def mode_terms(inv_time, modal_weight, state, length, backward):
    offsets = lax.broadcasted_iota(jnp.float32, (length, 1), 0)

    def one_mode(carry, pieces):
        rate_row, weight_row, state_row = pieces
        decay = jnp.exp(-offsets * rate_row[None, :])
        step_decay = (weight_row * jnp.exp(-rate_row))[None, :]
        term = step_decay * (decay[::-1] if backward else decay) * state_row[None, :]
        return (carry + term, None)

    start_terms = jnp.zeros((length, inv_time.shape[1]), jnp.float32)
    return lax.scan(one_mode, start_terms, (inv_time, modal_weight, state))[0]


def body(
    gate_input,
    key_input,
    value_input,
    short_filters,
    pole_time,
    residues,
    out_weight,
    out_cotangent,
):
    length = gate_input.shape[0]
    tap_count = short_filters.shape[1]
    half = out_weight.shape[1] // 2
    weight_left = lax.all_gather(out_weight[:, :half], "ctx", axis=0, tiled=True)
    weight_right = gather_ctx(out_weight[:, half:]).reshape(-1, half)
    stacked = jnp.stack([gate_input, key_input, value_input])
    tails = from_behind(stacked[:, length - (tap_count - 1) :, :], "ctx", 1)
    extended = jnp.concatenate([tails, stacked], axis=1).astype(jnp.float32)
    gate_short = causal_taps(extended[0], short_filters[0], length)
    key_short = causal_taps(extended[1], short_filters[1], length)
    value_short = causal_taps(extended[2], short_filters[2], length)
    mixed = key_short * value_short
    inv_time = 1.0 / pole_time.T
    modal_weight = residues.T * jnp.sqrt(-jnp.expm1(-2.0 * inv_time))
    block_decay = jnp.exp(-float(length) * inv_time)
    filt_table, forward_sums = mode_sums(inv_time, modal_weight, mixed, length)
    state_in = carried_in(gather_ctx(forward_sums), block_decay, False)
    forward, inverse = spectral_tables(length)
    spectrum = jnp.dot(forward, filt_table, precision=HIGHEST)
    long_local = apply_filter(spectrum, mixed, forward, inverse)
    long_out = long_local + mode_terms(inv_time, modal_weight, state_in, length, False)
    gated = (gate_short * long_out).astype(jnp.bfloat16)
    gated_full = lax.all_gather(gated, "chan", axis=1, tiled=True)
    contract = (((1,), (1,)), ((), ()))
    partial = lax.dot_general(
        weight_left, out_cotangent[:, :half], contract, preferred_element_type=jnp.float32
    ) + lax.dot_general(
        weight_right, out_cotangent[:, half:], contract, preferred_element_type=jnp.float32
    )
    partial, _ = lax.optimization_barrier((partial, gated))
    grad_gated = reduce_chan(partial).T
    grad_long = grad_gated * gate_short
    backward_sums = mode_sums_back(inv_time, grad_long, length)
    state_back = carried_in(gather_ctx(backward_sums), block_decay, True)
    back_local = apply_filter(spectrum, grad_long[::-1], forward, inverse)[::-1]
    grad_mixed = back_local + mode_terms(inv_time, modal_weight, state_back, length, True)
    block_output = jnp.concatenate(
        [
            jnp.dot(gated_full, weight_left, preferred_element_type=jnp.float32),
            jnp.dot(gated_full, weight_right, preferred_element_type=jnp.float32),
        ],
        axis=1,
    ).astype(jnp.bfloat16)
    grad_gate_short = grad_gated * long_out
    grad_key_short = grad_mixed * value_short
    grad_value_short = grad_mixed * key_short
    grads = jnp.stack([grad_gate_short, grad_key_short, grad_value_short])
    heads = from_behind(grads[:, : tap_count - 1, :], "ctx", -1)
    ext_grads = jnp.concatenate([grads, heads], axis=1)
    gate_grad = anti_taps(ext_grads[0], short_filters[0], length).astype(jnp.bfloat16)
    key_grad = anti_taps(ext_grads[1], short_filters[1], length).astype(jnp.bfloat16)
    value_grad = anti_taps(ext_grads[2], short_filters[2], length).astype(jnp.bfloat16)
    return (block_output, gate_grad, key_grad, value_grad)


def solution(mesh):
    in_specs = (
        P("ctx", "chan"),
        P("ctx", "chan"),
        P("ctx", "chan"),
        P(None, None, "chan"),
        P("chan", None),
        P("chan", None),
        P("ctx", "chan"),
        P("ctx", "chan"),
    )
    out_specs = (P("ctx", "chan"), P("ctx", "chan"), P("ctx", "chan"), P("ctx", "chan"))
    return jax.shard_map(body, mesh=mesh, in_specs=in_specs, out_specs=out_specs, check_vma=False)
```

```python
import math

import jax
import jax.numpy as jnp
from jax import lax
from jax.sharding import PartitionSpec as P

HIGHEST = lax.Precision.HIGHEST


def from_behind(block, axis, distance):
    devices = range(lax.axis_size(axis))
    route = [(i - distance, i) for i in devices if i - distance in devices]
    return lax.ppermute(block, axis, route)


def gather_ctx(block):
    peers, position = (lax.axis_size("ctx"), lax.axis_index("ctx"))
    recv = [block] + [
        lax.ppermute(block, "ctx", [(i, (i + d) % peers) for i in range(peers)])
        for d in range(1, peers)
    ]
    order = (position - jnp.arange(peers)) % peers
    return jnp.take(jnp.stack(recv), order, axis=0)


def gather_chan(block):
    peers, position = (lax.axis_size("chan"), lax.axis_index("chan"))
    groups = [list(range(b, peers, 2)) for b in range(2)]
    mine = lax.all_gather(block, "chan", axis=0, axis_index_groups=groups)
    theirs = lax.ppermute(mine, "chan", [(j, j ^ 1) for j in range(peers)])
    low = position % 2 == 0
    pairs = jnp.stack([jnp.where(low, mine, theirs), jnp.where(low, theirs, mine)], axis=1)
    return jnp.transpose(pairs, (2, 0, 1, 3)).reshape(block.shape[0], -1)


def reduce_chan(partial):
    peers, position = (lax.axis_size("chan"), lax.axis_index("chan"))
    chunks = partial.reshape(peers // 2, 2, -1, partial.shape[1])
    keep = lax.dynamic_index_in_dim(chunks, position % 2, axis=1, keepdims=False)
    give = lax.dynamic_index_in_dim(chunks, 1 - position % 2, axis=1, keepdims=False)
    half = keep + lax.ppermute(give, "chan", [(j, j ^ 1) for j in range(peers)])
    groups = [list(range(b, peers, 2)) for b in range(2)]
    arrived = lax.all_to_all(half, "chan", 0, 0, axis_index_groups=groups, tiled=True)
    return jnp.sum(arrived, axis=0)


def carried_in(every, block_decay, reverse):
    peers, position = (every.shape[0], lax.axis_index("ctx"))
    state = jnp.zeros_like(block_decay)
    for at in range(peers - 1, -1, -1) if reverse else range(peers):
        reached = at > position if reverse else at < position
        state = jnp.where(reached, block_decay * state + every[at], state)
    return state


def causal_taps(extended, filter_taps, length):
    tap_count = filter_taps.shape[0]
    summed = jnp.zeros((length, extended.shape[1]), jnp.float32)
    for offset in range(tap_count):
        lead_row = tap_count - 1 - offset
        summed = summed + filter_taps[offset][None, :] * extended[lead_row : lead_row + length]
    return summed


def anti_taps(extended, filter_taps, length):
    tap_count = filter_taps.shape[0]
    summed = jnp.zeros((length, extended.shape[1]), jnp.float32)
    for offset in range(tap_count):
        summed = summed + filter_taps[offset][None, :] * extended[offset : offset + length]
    return summed


def spectral_tables(length):
    doubled = 2 * length
    freqs = lax.broadcasted_iota(jnp.int32, (doubled, length), 0)
    places = lax.broadcasted_iota(jnp.int32, (doubled, length), 1)
    angles = (freqs * places % doubled).astype(jnp.float32) * (2.0 * math.pi / doubled)
    forward = jnp.concatenate([jnp.cos(angles), -jnp.sin(angles)], axis=0)
    inverse = forward.T / doubled
    return (forward, inverse)


def apply_filter(spectrum, signal, forward, inverse):
    middle = forward.shape[0] // 2
    spectra = jnp.dot(forward, signal, precision=HIGHEST)
    real_sig = spectra[:middle]
    imag_sig = spectra[middle:]
    real_filt = spectrum[:middle]
    imag_filt = spectrum[middle:]
    product = jnp.concatenate(
        [real_sig * real_filt - imag_sig * imag_filt, real_sig * imag_filt + imag_sig * real_filt],
        axis=0,
    )
    return jnp.dot(inverse, product, precision=HIGHEST)


def mode_sums(inv_time, modal_weight, mixed, length):
    offsets = lax.broadcasted_iota(jnp.float32, (length, 1), 0)

    def one_mode(carry, pieces):
        rate_row, weight_row = pieces
        decay = jnp.exp(-offsets * rate_row[None, :])
        forward_sum = jnp.sum(decay[::-1] * mixed, axis=0)
        return (carry + weight_row[None, :] * decay, forward_sum)

    start_filter = jnp.zeros((length, mixed.shape[1]), jnp.float32)
    return lax.scan(one_mode, start_filter, (inv_time, modal_weight))


def mode_sums_back(inv_time, grad_long, length):
    offsets = lax.broadcasted_iota(jnp.float32, (length, 1), 0)

    def one_mode(carry, rate_row):
        decay = jnp.exp(-offsets * rate_row[None, :])
        return (carry, jnp.sum(decay * grad_long, axis=0))

    return lax.scan(one_mode, 0, inv_time)[1]


def mode_terms(inv_time, modal_weight, state, length, backward):
    offsets = lax.broadcasted_iota(jnp.float32, (length, 1), 0)

    def one_mode(carry, pieces):
        rate_row, weight_row, state_row = pieces
        decay = jnp.exp(-offsets * rate_row[None, :])
        step_decay = (weight_row * jnp.exp(-rate_row))[None, :]
        term = step_decay * (decay[::-1] if backward else decay) * state_row[None, :]
        return (carry + term, None)

    start_terms = jnp.zeros((length, inv_time.shape[1]), jnp.float32)
    return lax.scan(one_mode, start_terms, (inv_time, modal_weight, state))[0]


def body(
    gate_input,
    key_input,
    value_input,
    short_filters,
    pole_time,
    residues,
    out_weight,
    out_cotangent,
):
    length = gate_input.shape[0]
    tap_count = short_filters.shape[1]
    half = out_weight.shape[1] // 2
    weight_left = lax.all_gather(out_weight[:, :half], "ctx", axis=0, tiled=True)
    weight_right = gather_ctx(out_weight[:, half:]).reshape(-1, half)
    stacked = jnp.stack([gate_input, key_input, value_input])
    tails = from_behind(stacked[:, length - (tap_count - 1) :, :], "ctx", 1)
    extended = jnp.concatenate([tails, stacked], axis=1).astype(jnp.float32)
    gate_short = causal_taps(extended[0], short_filters[0], length)
    key_short = causal_taps(extended[1], short_filters[1], length)
    value_short = causal_taps(extended[2], short_filters[2], length)
    mixed = key_short * value_short
    inv_time = 1.0 / pole_time.T
    modal_weight = residues.T * jnp.sqrt(-jnp.expm1(-2.0 * inv_time))
    block_decay = jnp.exp(-float(length) * inv_time)
    filt_table, forward_sums = mode_sums(inv_time, modal_weight, mixed, length)
    state_in = carried_in(gather_ctx(forward_sums), block_decay, False)
    forward, inverse = spectral_tables(length)
    spectrum = jnp.dot(forward, filt_table, precision=HIGHEST)
    long_local = apply_filter(spectrum, mixed, forward, inverse)
    long_out = long_local + mode_terms(inv_time, modal_weight, state_in, length, False)
    gated = (gate_short * long_out).astype(jnp.bfloat16)
    gated_full = gather_chan(gated)
    contract = (((1,), (1,)), ((), ()))
    partial = lax.dot_general(
        weight_left, out_cotangent[:, :half], contract, preferred_element_type=jnp.float32
    ) + lax.dot_general(
        weight_right, out_cotangent[:, half:], contract, preferred_element_type=jnp.float32
    )
    partial, _ = lax.optimization_barrier((partial, gated))
    grad_gated = reduce_chan(partial).T
    grad_long = grad_gated * gate_short
    backward_sums = mode_sums_back(inv_time, grad_long, length)
    state_back = carried_in(gather_ctx(backward_sums), block_decay, True)
    back_local = apply_filter(spectrum, grad_long[::-1], forward, inverse)[::-1]
    grad_mixed = back_local + mode_terms(inv_time, modal_weight, state_back, length, True)
    block_output = jnp.concatenate(
        [
            jnp.dot(gated_full, weight_left, preferred_element_type=jnp.float32),
            jnp.dot(gated_full, weight_right, preferred_element_type=jnp.float32),
        ],
        axis=1,
    ).astype(jnp.bfloat16)
    grad_gate_short = grad_gated * long_out
    grad_key_short = grad_mixed * value_short
    grad_value_short = grad_mixed * key_short
    grads = jnp.stack([grad_gate_short, grad_key_short, grad_value_short])
    heads = from_behind(grads[:, : tap_count - 1, :], "ctx", -1)
    ext_grads = jnp.concatenate([grads, heads], axis=1)
    gate_grad = anti_taps(ext_grads[0], short_filters[0], length).astype(jnp.bfloat16)
    key_grad = anti_taps(ext_grads[1], short_filters[1], length).astype(jnp.bfloat16)
    value_grad = anti_taps(ext_grads[2], short_filters[2], length).astype(jnp.bfloat16)
    return (block_output, gate_grad, key_grad, value_grad)


def solution(mesh):
    in_specs = (
        P("ctx", "chan"),
        P("ctx", "chan"),
        P("ctx", "chan"),
        P(None, None, "chan"),
        P("chan", None),
        P("chan", None),
        P("ctx", "chan"),
        P("ctx", "chan"),
    )
    out_specs = (P("ctx", "chan"), P("ctx", "chan"), P("ctx", "chan"), P("ctx", "chan"))
    return jax.shard_map(body, mesh=mesh, in_specs=in_specs, out_specs=out_specs, check_vma=False)
```

```python
import math

import jax
import jax.numpy as jnp
from jax import lax
from jax.sharding import PartitionSpec as P

HIGHEST = lax.Precision.HIGHEST


def from_behind(block, axis, distance):
    devices = range(lax.axis_size(axis))
    route = [(i - distance, i) for i in devices if i - distance in devices]
    return lax.ppermute(block, axis, route)


def gather_ctx(block):
    peers, position = (lax.axis_size("ctx"), lax.axis_index("ctx"))
    recv = [block] + [
        lax.ppermute(block, "ctx", [(i, (i + d) % peers) for i in range(peers)])
        for d in range(1, peers)
    ]
    order = (position - jnp.arange(peers)) % peers
    return jnp.take(jnp.stack(recv), order, axis=0)


def reduce_chan(partial):
    peers, position = (lax.axis_size("chan"), lax.axis_index("chan"))
    chunks = partial.reshape(peers // 2, 2, -1, partial.shape[1])
    keep = lax.dynamic_index_in_dim(chunks, position % 2, axis=1, keepdims=False)
    give = lax.dynamic_index_in_dim(chunks, 1 - position % 2, axis=1, keepdims=False)
    half = keep + lax.ppermute(give, "chan", [(j, j ^ 1) for j in range(peers)])
    groups = [list(range(b, peers, 2)) for b in range(2)]
    arrived = lax.all_to_all(half, "chan", 0, 0, axis_index_groups=groups, tiled=True)
    return jnp.sum(arrived, axis=0)


def carried_in(every, block_decay, reverse):
    peers, position = (every.shape[0], lax.axis_index("ctx"))
    state = jnp.zeros_like(block_decay)
    for at in range(peers - 1, -1, -1) if reverse else range(peers):
        reached = at > position if reverse else at < position
        state = jnp.where(reached, block_decay * state + every[at], state)
    return state


def causal_taps(extended, filter_taps, length):
    tap_count = filter_taps.shape[0]
    summed = jnp.zeros((length, extended.shape[1]), jnp.float32)
    for offset in range(tap_count):
        lead_row = tap_count - 1 - offset
        summed = summed + filter_taps[offset][None, :] * extended[lead_row : lead_row + length]
    return summed


def anti_taps(extended, filter_taps, length):
    tap_count = filter_taps.shape[0]
    summed = jnp.zeros((length, extended.shape[1]), jnp.float32)
    for offset in range(tap_count):
        summed = summed + filter_taps[offset][None, :] * extended[offset : offset + length]
    return summed


def spectral_tables(length):
    doubled = 2 * length
    freqs = lax.broadcasted_iota(jnp.int32, (doubled, length), 0)
    places = lax.broadcasted_iota(jnp.int32, (doubled, length), 1)
    angles = (freqs * places % doubled).astype(jnp.float32) * (2.0 * math.pi / doubled)
    forward = jnp.concatenate([jnp.cos(angles), -jnp.sin(angles)], axis=0)
    inverse = forward.T / doubled
    return (forward, inverse)


def apply_filter(spectrum, signal, forward, inverse):
    middle = forward.shape[0] // 2
    spectra = jnp.dot(forward, signal, precision=HIGHEST)
    real_sig = spectra[:middle]
    imag_sig = spectra[middle:]
    real_filt = spectrum[:middle]
    imag_filt = spectrum[middle:]
    product = jnp.concatenate(
        [real_sig * real_filt - imag_sig * imag_filt, real_sig * imag_filt + imag_sig * real_filt],
        axis=0,
    )
    return jnp.dot(inverse, product, precision=HIGHEST)


def mode_sums(inv_time, modal_weight, mixed, length):
    offsets = lax.broadcasted_iota(jnp.float32, (length, 1), 0)

    def one_mode(carry, pieces):
        rate_row, weight_row = pieces
        decay = jnp.exp(-offsets * rate_row[None, :])
        forward_sum = jnp.sum(decay[::-1] * mixed, axis=0)
        return (carry + weight_row[None, :] * decay, forward_sum)

    start_filter = jnp.zeros((length, mixed.shape[1]), jnp.float32)
    return lax.scan(one_mode, start_filter, (inv_time, modal_weight))


def mode_sums_back(inv_time, grad_long, length):
    offsets = lax.broadcasted_iota(jnp.float32, (length, 1), 0)

    def one_mode(carry, rate_row):
        decay = jnp.exp(-offsets * rate_row[None, :])
        return (carry, jnp.sum(decay * grad_long, axis=0))

    return lax.scan(one_mode, 0, inv_time)[1]


def mode_terms(inv_time, modal_weight, state, length, backward):
    offsets = lax.broadcasted_iota(jnp.float32, (length, 1), 0)

    def one_mode(carry, pieces):
        rate_row, weight_row, state_row = pieces
        decay = jnp.exp(-offsets * rate_row[None, :])
        step_decay = (weight_row * jnp.exp(-rate_row))[None, :]
        term = step_decay * (decay[::-1] if backward else decay) * state_row[None, :]
        return (carry + term, None)

    start_terms = jnp.zeros((length, inv_time.shape[1]), jnp.float32)
    return lax.scan(one_mode, start_terms, (inv_time, modal_weight, state))[0]


def body(
    gate_input,
    key_input,
    value_input,
    short_filters,
    pole_time,
    residues,
    out_weight,
    out_cotangent,
):
    length = gate_input.shape[0]
    tap_count = short_filters.shape[1]
    half = out_weight.shape[1] // 2
    weight_left = lax.all_gather(out_weight[:, :half], "ctx", axis=0, tiled=True)
    weight_right = gather_ctx(out_weight[:, half:]).reshape(-1, half)
    stacked = jnp.stack([gate_input, key_input, value_input])
    tails = from_behind(stacked[:, length - (tap_count - 1) :, :], "ctx", 1)
    extended = jnp.concatenate([tails, stacked], axis=1).astype(jnp.float32)
    gate_short = causal_taps(extended[0], short_filters[0], length)
    key_short = causal_taps(extended[1], short_filters[1], length)
    value_short = causal_taps(extended[2], short_filters[2], length)
    mixed = key_short * value_short
    inv_time = 1.0 / pole_time.T
    modal_weight = residues.T * jnp.sqrt(-jnp.expm1(-2.0 * inv_time))
    block_decay = jnp.exp(-float(length) * inv_time)
    filt_table, forward_sums = mode_sums(inv_time, modal_weight, mixed, length)
    state_in = carried_in(gather_ctx(forward_sums), block_decay, False)
    forward, inverse = spectral_tables(length)
    spectrum = jnp.dot(forward, filt_table, precision=HIGHEST)
    long_local = apply_filter(spectrum, mixed, forward, inverse)
    long_out = long_local + mode_terms(inv_time, modal_weight, state_in, length, False)
    gated = (gate_short * long_out).astype(jnp.bfloat16)
    copies = jnp.broadcast_to(gated[None], (lax.axis_size("chan"),) + gated.shape)
    arrived_gated = lax.all_to_all(copies, "chan", 0, 0, tiled=True)
    gated_full = jnp.transpose(arrived_gated, (1, 0, 2)).reshape(gated.shape[0], -1)
    contract = (((1,), (1,)), ((), ()))
    partial = lax.dot_general(
        weight_left, out_cotangent[:, :half], contract, preferred_element_type=jnp.float32
    ) + lax.dot_general(
        weight_right, out_cotangent[:, half:], contract, preferred_element_type=jnp.float32
    )
    partial, _ = lax.optimization_barrier((partial, gated))
    grad_gated = reduce_chan(partial).T
    grad_long = grad_gated * gate_short
    backward_sums = mode_sums_back(inv_time, grad_long, length)
    state_back = carried_in(gather_ctx(backward_sums), block_decay, True)
    back_local = apply_filter(spectrum, grad_long[::-1], forward, inverse)[::-1]
    grad_mixed = back_local + mode_terms(inv_time, modal_weight, state_back, length, True)
    block_output = jnp.concatenate(
        [
            jnp.dot(gated_full, weight_left, preferred_element_type=jnp.float32),
            jnp.dot(gated_full, weight_right, preferred_element_type=jnp.float32),
        ],
        axis=1,
    ).astype(jnp.bfloat16)
    grad_gate_short = grad_gated * long_out
    grad_key_short = grad_mixed * value_short
    grad_value_short = grad_mixed * key_short
    grads = jnp.stack([grad_gate_short, grad_key_short, grad_value_short])
    heads = from_behind(grads[:, : tap_count - 1, :], "ctx", -1)
    ext_grads = jnp.concatenate([grads, heads], axis=1)
    gate_grad = anti_taps(ext_grads[0], short_filters[0], length).astype(jnp.bfloat16)
    key_grad = anti_taps(ext_grads[1], short_filters[1], length).astype(jnp.bfloat16)
    value_grad = anti_taps(ext_grads[2], short_filters[2], length).astype(jnp.bfloat16)
    return (block_output, gate_grad, key_grad, value_grad)


def solution(mesh):
    in_specs = (
        P("ctx", "chan"),
        P("ctx", "chan"),
        P("ctx", "chan"),
        P(None, None, "chan"),
        P("chan", None),
        P("chan", None),
        P("ctx", "chan"),
        P("ctx", "chan"),
    )
    out_specs = (P("ctx", "chan"), P("ctx", "chan"), P("ctx", "chan"), P("ctx", "chan"))
    return jax.shard_map(body, mesh=mesh, in_specs=in_specs, out_specs=out_specs, check_vma=False)
```

```python
import math

import jax
import jax.numpy as jnp
from jax import lax
from jax.sharding import PartitionSpec as P

HIGHEST = lax.Precision.HIGHEST


def from_behind(block, axis, distance):
    devices = range(lax.axis_size(axis))
    route = [(i - distance, i) for i in devices if i - distance in devices]
    return lax.ppermute(block, axis, route)


def gather_ctx(block):
    peers, position = (lax.axis_size("ctx"), lax.axis_index("ctx"))
    recv = [block] + [
        lax.ppermute(block, "ctx", [(i, (i + d) % peers) for i in range(peers)])
        for d in range(1, peers)
    ]
    order = (position - jnp.arange(peers)) % peers
    return jnp.take(jnp.stack(recv), order, axis=0, mode="clip")


def reduce_chan(partial):
    peers, position = (lax.axis_size("chan"), lax.axis_index("chan"))
    chunks = partial.reshape(peers // 2, 2, -1, partial.shape[1])
    keep = lax.dynamic_index_in_dim(chunks, position % 2, axis=1, keepdims=False)
    give = lax.dynamic_index_in_dim(chunks, 1 - position % 2, axis=1, keepdims=False)
    half = keep + lax.ppermute(give, "chan", [(j, j ^ 1) for j in range(peers)])
    groups = [list(range(b, peers, 2)) for b in range(2)]
    arrived = lax.all_to_all(half, "chan", 0, 0, axis_index_groups=groups, tiled=True)
    return jnp.sum(arrived, axis=0)


def carried_in(sums, block_decay, reverse):
    peers = lax.axis_size("ctx")
    state = jnp.zeros_like(block_decay)
    for d in range(peers - 1, 0, -1):
        route = [(i + d, i) if reverse else (i, i + d) for i in range(peers - d)]
        state = block_decay * state + lax.ppermute(sums, "ctx", route)
    return state


def causal_taps(extended, filter_taps, length):
    tap_count = filter_taps.shape[0]
    summed = jnp.zeros((length, extended.shape[1]), jnp.float32)
    for offset in range(tap_count):
        lead_row = tap_count - 1 - offset
        summed = summed + filter_taps[offset][None, :] * extended[lead_row : lead_row + length]
    return summed


def anti_taps(extended, filter_taps, length):
    tap_count = filter_taps.shape[0]
    summed = jnp.zeros((length, extended.shape[1]), jnp.float32)
    for offset in range(tap_count):
        summed = summed + filter_taps[offset][None, :] * extended[offset : offset + length]
    return summed


def spectral_tables(length):
    doubled = 2 * length
    freqs = lax.broadcasted_iota(jnp.int32, (doubled, length), 0)
    places = lax.broadcasted_iota(jnp.int32, (doubled, length), 1)
    angles = (freqs * places % doubled).astype(jnp.float32) * (2.0 * math.pi / doubled)
    forward = jnp.concatenate([jnp.cos(angles), -jnp.sin(angles)], axis=0)
    inverse = forward.T / doubled
    return (forward, inverse)


def apply_filter(spectrum, signal, forward, inverse):
    middle = forward.shape[0] // 2
    spectra = jnp.dot(forward, signal, precision=HIGHEST)
    real_sig = spectra[:middle]
    imag_sig = spectra[middle:]
    real_filt = spectrum[:middle]
    imag_filt = spectrum[middle:]
    product = jnp.concatenate(
        [real_sig * real_filt - imag_sig * imag_filt, real_sig * imag_filt + imag_sig * real_filt],
        axis=0,
    )
    return jnp.dot(inverse, product, precision=HIGHEST)


def mode_decay(inv_time, length):
    offsets = lax.broadcasted_iota(jnp.float32, (1, length, 1), 1)
    return jnp.exp(-offsets * inv_time[:, None, :])


def mode_sums(decay, modal_weight, mixed):
    forward_sums = jnp.sum(decay[:, ::-1, :] * mixed[None], axis=1)
    return (jnp.sum(modal_weight[:, None, :] * decay, axis=0), forward_sums)


def mode_sums_back(decay, grad_long):
    return jnp.sum(decay * grad_long[None], axis=1)


def mode_terms(decay, inv_time, modal_weight, state, backward):
    step_decay = (modal_weight * jnp.exp(-inv_time))[:, None, :]
    term = step_decay * (decay[:, ::-1, :] if backward else decay) * state[:, None, :]
    return jnp.sum(term, axis=0)


def body(
    gate_input,
    key_input,
    value_input,
    short_filters,
    pole_time,
    residues,
    out_weight,
    out_cotangent,
):
    length = gate_input.shape[0]
    tap_count = short_filters.shape[1]
    half = out_weight.shape[1] // 2
    weight_left = lax.all_gather(out_weight[:, :half], "ctx", axis=0, tiled=True)
    weight_right = gather_ctx(out_weight[:, half:]).reshape(-1, half)
    stacked = jnp.stack([gate_input, key_input, value_input])
    tails = from_behind(stacked[:, length - (tap_count - 1) :, :], "ctx", 1)
    extended = jnp.concatenate([tails, stacked], axis=1).astype(jnp.float32)
    gate_short = causal_taps(extended[0], short_filters[0], length)
    key_short = causal_taps(extended[1], short_filters[1], length)
    value_short = causal_taps(extended[2], short_filters[2], length)
    mixed = key_short * value_short
    inv_time = 1.0 / pole_time.T
    modal_weight = residues.T * jnp.sqrt(-jnp.expm1(-2.0 * inv_time))
    block_decay = jnp.exp(-float(length) * inv_time)
    decay = mode_decay(inv_time, length)
    filt_table, forward_sums = mode_sums(decay, modal_weight, mixed)
    state_in = carried_in(forward_sums, block_decay, False)
    forward, inverse = spectral_tables(length)
    spectrum = jnp.dot(forward, filt_table, precision=HIGHEST)
    long_local = apply_filter(spectrum, mixed, forward, inverse)
    long_out = long_local + mode_terms(decay, inv_time, modal_weight, state_in, False)
    gated = (gate_short * long_out).astype(jnp.bfloat16)
    copies = jnp.broadcast_to(gated[None], (lax.axis_size("chan"),) + gated.shape)
    arrived_gated = lax.all_to_all(copies, "chan", 0, 0, tiled=True)
    gated_full = jnp.transpose(arrived_gated, (1, 0, 2)).reshape(gated.shape[0], -1)
    contract = (((1,), (1,)), ((), ()))
    partial = lax.dot_general(
        weight_left, out_cotangent[:, :half], contract, preferred_element_type=jnp.float32
    ) + lax.dot_general(
        weight_right, out_cotangent[:, half:], contract, preferred_element_type=jnp.float32
    )
    partial, _ = lax.optimization_barrier((partial, gated))
    grad_gated = reduce_chan(partial).T
    grad_long = grad_gated * gate_short
    backward_sums = mode_sums_back(decay, grad_long)
    state_back = carried_in(backward_sums, block_decay, True)
    back_local = apply_filter(spectrum, grad_long[::-1], forward, inverse)[::-1]
    grad_mixed = back_local + mode_terms(decay, inv_time, modal_weight, state_back, True)
    block_output = jnp.concatenate(
        [
            jnp.dot(gated_full, weight_left, preferred_element_type=jnp.float32),
            jnp.dot(gated_full, weight_right, preferred_element_type=jnp.float32),
        ],
        axis=1,
    ).astype(jnp.bfloat16)
    grad_gate_short = grad_gated * long_out
    grad_key_short = grad_mixed * value_short
    grad_value_short = grad_mixed * key_short
    grads = jnp.stack([grad_gate_short, grad_key_short, grad_value_short])
    heads = from_behind(grads[:, : tap_count - 1, :], "ctx", -1)
    ext_grads = jnp.concatenate([grads, heads], axis=1)
    gate_grad = anti_taps(ext_grads[0], short_filters[0], length).astype(jnp.bfloat16)
    key_grad = anti_taps(ext_grads[1], short_filters[1], length).astype(jnp.bfloat16)
    value_grad = anti_taps(ext_grads[2], short_filters[2], length).astype(jnp.bfloat16)
    return (block_output, gate_grad, key_grad, value_grad)


def solution(mesh):
    in_specs = (
        P("ctx", "chan"),
        P("ctx", "chan"),
        P("ctx", "chan"),
        P(None, None, "chan"),
        P("chan", None),
        P("chan", None),
        P("ctx", "chan"),
        P("ctx", "chan"),
    )
    out_specs = (P("ctx", "chan"), P("ctx", "chan"), P("ctx", "chan"), P("ctx", "chan"))
    return jax.shard_map(body, mesh=mesh, in_specs=in_specs, out_specs=out_specs, check_vma=False)
```

```python
import math

import jax
import jax.numpy as jnp
from jax import lax
from jax.sharding import PartitionSpec as P

HIGHEST = lax.Precision.HIGHEST


def from_behind(block, axis, distance):
    devices = range(lax.axis_size(axis))
    route = [(i - distance, i) for i in devices if i - distance in devices]
    return lax.ppermute(block, axis, route)


def gather_ctx(block):
    peers, position = (lax.axis_size("ctx"), lax.axis_index("ctx"))
    recv = [block] + [
        lax.ppermute(block, "ctx", [(i, (i + d) % peers) for i in range(peers)])
        for d in range(1, peers)
    ]
    order = (position - jnp.arange(peers)) % peers
    return jnp.take(jnp.stack(recv), order, axis=0, mode="clip")


def reduce_chan(partial):
    peers, position = (lax.axis_size("chan"), lax.axis_index("chan"))
    chunks = partial.reshape(peers // 2, 2, -1, partial.shape[1])
    keep = lax.dynamic_index_in_dim(chunks, position % 2, axis=1, keepdims=False)
    give = lax.dynamic_index_in_dim(chunks, 1 - position % 2, axis=1, keepdims=False)
    half = keep + lax.ppermute(give, "chan", [(j, j ^ 1) for j in range(peers)])
    groups = [list(range(b, peers, 2)) for b in range(2)]
    arrived = lax.all_to_all(half, "chan", 0, 0, axis_index_groups=groups, tiled=True)
    return jnp.sum(arrived, axis=0)


def carried_in(sums, block_decay, reverse):
    peers = lax.axis_size("ctx")
    state = jnp.zeros_like(block_decay)
    for d in range(peers - 1, 0, -1):
        route = [(i + d, i) if reverse else (i, i + d) for i in range(peers - d)]
        state = block_decay * state + lax.ppermute(sums, "ctx", route)
    return state


def causal_taps(extended, filter_taps, length):
    tap_count = filter_taps.shape[0]
    summed = jnp.zeros((length, extended.shape[1]), jnp.float32)
    for offset in range(tap_count):
        lead_row = tap_count - 1 - offset
        summed = summed + filter_taps[offset][None, :] * extended[lead_row : lead_row + length]
    return summed


def anti_taps(extended, filter_taps, length):
    tap_count = filter_taps.shape[0]
    summed = jnp.zeros((length, extended.shape[1]), jnp.float32)
    for offset in range(tap_count):
        summed = summed + filter_taps[offset][None, :] * extended[offset : offset + length]
    return summed


def spectral_tables(length):
    doubled = 2 * length
    freqs = lax.broadcasted_iota(jnp.int32, (doubled, length), 0)
    places = lax.broadcasted_iota(jnp.int32, (doubled, length), 1)
    angles = (freqs * places % doubled).astype(jnp.float32) * (2.0 * math.pi / doubled)
    forward = jnp.concatenate([jnp.cos(angles), -jnp.sin(angles)], axis=0)
    inverse = forward.T / doubled
    return (forward, inverse)


def apply_filter(spectrum, signal, forward, inverse):
    middle = forward.shape[0] // 2
    spectra = jnp.dot(forward, signal, precision=HIGHEST)
    real_sig = spectra[:middle]
    imag_sig = spectra[middle:]
    real_filt = spectrum[:middle]
    imag_filt = spectrum[middle:]
    product = jnp.concatenate(
        [real_sig * real_filt - imag_sig * imag_filt, real_sig * imag_filt + imag_sig * real_filt],
        axis=0,
    )
    return jnp.dot(inverse, product, precision=HIGHEST)


def mode_decay(inv_time, length, backward):
    offsets = lax.broadcasted_iota(jnp.float32, (1, length, 1), 1)
    if backward:
        offsets = float(length - 1) - offsets
    return jnp.exp(-offsets * inv_time[:, None, :])


def mode_sums(decay, decay_back, modal_weight, mixed):
    forward_sums = jnp.sum(decay_back * mixed[None], axis=1)
    return (jnp.sum(modal_weight[:, None, :] * decay, axis=0), forward_sums)


def mode_sums_back(decay, grad_long):
    return jnp.sum(decay * grad_long[None], axis=1)


def mode_terms(decay, inv_time, modal_weight, state):
    step_decay = (modal_weight * jnp.exp(-inv_time))[:, None, :]
    term = step_decay * decay * state[:, None, :]
    return jnp.sum(term, axis=0)


def body(
    gate_input,
    key_input,
    value_input,
    short_filters,
    pole_time,
    residues,
    out_weight,
    out_cotangent,
):
    length = gate_input.shape[0]
    tap_count = short_filters.shape[1]
    half = out_weight.shape[1] // 2
    weight_left = lax.all_gather(out_weight[:, :half], "ctx", axis=0, tiled=True)
    weight_right = gather_ctx(out_weight[:, half:]).reshape(-1, half)
    stacked = jnp.stack([gate_input, key_input, value_input])
    tails = from_behind(stacked[:, length - (tap_count - 1) :, :], "ctx", 1)
    extended = jnp.concatenate([tails, stacked], axis=1).astype(jnp.float32)
    gate_short = causal_taps(extended[0], short_filters[0], length)
    key_short = causal_taps(extended[1], short_filters[1], length)
    value_short = causal_taps(extended[2], short_filters[2], length)
    mixed = key_short * value_short
    inv_time = 1.0 / pole_time.T
    modal_weight = residues.T * jnp.sqrt(-jnp.expm1(-2.0 * inv_time))
    block_decay = jnp.exp(-float(length) * inv_time)
    decay = mode_decay(inv_time, length, False)
    decay_back = mode_decay(inv_time, length, True)
    filt_table, forward_sums = mode_sums(decay, decay_back, modal_weight, mixed)
    state_in = carried_in(forward_sums, block_decay, False)
    forward, inverse = spectral_tables(length)
    spectrum = jnp.dot(forward, filt_table, precision=HIGHEST)
    long_local = apply_filter(spectrum, mixed, forward, inverse)
    long_out = long_local + mode_terms(decay, inv_time, modal_weight, state_in)
    gated = (gate_short * long_out).astype(jnp.bfloat16)
    copies = jnp.broadcast_to(gated[None], (lax.axis_size("chan"),) + gated.shape)
    arrived_gated = lax.all_to_all(copies, "chan", 0, 0, tiled=True)
    gated_full = jnp.transpose(arrived_gated, (1, 0, 2)).reshape(gated.shape[0], -1)
    contract = (((1,), (1,)), ((), ()))
    partial = lax.dot_general(
        weight_left, out_cotangent[:, :half], contract, preferred_element_type=jnp.float32
    ) + lax.dot_general(
        weight_right, out_cotangent[:, half:], contract, preferred_element_type=jnp.float32
    )
    partial, _ = lax.optimization_barrier((partial, gated))
    grad_gated = reduce_chan(partial).T
    grad_long = grad_gated * gate_short
    backward_sums = mode_sums_back(decay, grad_long)
    state_back = carried_in(backward_sums, block_decay, True)
    back_local = apply_filter(spectrum, grad_long[::-1], forward, inverse)[::-1]
    grad_mixed = back_local + mode_terms(decay_back, inv_time, modal_weight, state_back)
    block_output = jnp.concatenate(
        [
            jnp.dot(gated_full, weight_left, preferred_element_type=jnp.float32),
            jnp.dot(gated_full, weight_right, preferred_element_type=jnp.float32),
        ],
        axis=1,
    ).astype(jnp.bfloat16)
    grad_gate_short = grad_gated * long_out
    grad_key_short = grad_mixed * value_short
    grad_value_short = grad_mixed * key_short
    grads = jnp.stack([grad_gate_short, grad_key_short, grad_value_short])
    heads = from_behind(grads[:, : tap_count - 1, :], "ctx", -1)
    ext_grads = jnp.concatenate([grads, heads], axis=1)
    gate_grad = anti_taps(ext_grads[0], short_filters[0], length).astype(jnp.bfloat16)
    key_grad = anti_taps(ext_grads[1], short_filters[1], length).astype(jnp.bfloat16)
    value_grad = anti_taps(ext_grads[2], short_filters[2], length).astype(jnp.bfloat16)
    return (block_output, gate_grad, key_grad, value_grad)


def solution(mesh):
    in_specs = (
        P("ctx", "chan"),
        P("ctx", "chan"),
        P("ctx", "chan"),
        P(None, None, "chan"),
        P("chan", None),
        P("chan", None),
        P("ctx", "chan"),
        P("ctx", "chan"),
    )
    out_specs = (P("ctx", "chan"), P("ctx", "chan"), P("ctx", "chan"), P("ctx", "chan"))
    return jax.shard_map(body, mesh=mesh, in_specs=in_specs, out_specs=out_specs, check_vma=False)
```

```python
import math

import jax
import jax.numpy as jnp
from jax import lax
from jax.sharding import PartitionSpec as P

HIGHEST = lax.Precision.HIGHEST


def from_behind(block, axis, distance):
    devices = range(lax.axis_size(axis))
    route = [(i - distance, i) for i in devices if i - distance in devices]
    return lax.ppermute(block, axis, route)


def gather_ctx(block):
    peers, position = (lax.axis_size("ctx"), lax.axis_index("ctx"))
    recv = [block] + [
        lax.ppermute(block, "ctx", [(i, (i + d) % peers) for i in range(peers)])
        for d in range(1, peers)
    ]
    order = (position - jnp.arange(peers)) % peers
    return jnp.take(jnp.stack(recv), order, axis=0, mode="clip")


def reduce_chan(partial):
    peers, position = (lax.axis_size("chan"), lax.axis_index("chan"))
    chunks = partial.reshape(peers // 2, 2, -1, partial.shape[1])
    keep = lax.dynamic_index_in_dim(chunks, position % 2, axis=1, keepdims=False)
    give = lax.dynamic_index_in_dim(chunks, 1 - position % 2, axis=1, keepdims=False)
    half = keep + lax.ppermute(give, "chan", [(j, j ^ 1) for j in range(peers)])
    groups = [list(range(b, peers, 2)) for b in range(2)]
    arrived = lax.all_to_all(half, "chan", 0, 0, axis_index_groups=groups, tiled=True)
    return jnp.sum(arrived, axis=0)


def carried_in(sums, block_decay, reverse):
    peers = lax.axis_size("ctx")
    state = jnp.zeros_like(block_decay)
    for d in range(peers - 1, 0, -1):
        route = [(i + d, i) if reverse else (i, i + d) for i in range(peers - d)]
        state = block_decay * state + lax.ppermute(sums, "ctx", route)
    return state


def causal_taps(extended, filter_taps, length):
    tap_count = filter_taps.shape[0]
    summed = jnp.zeros((length, extended.shape[1]), jnp.float32)
    for offset in range(tap_count):
        lead_row = tap_count - 1 - offset
        summed = summed + filter_taps[offset][None, :] * extended[lead_row : lead_row + length]
    return summed


def anti_taps(extended, filter_taps, length):
    tap_count = filter_taps.shape[0]
    summed = jnp.zeros((length, extended.shape[1]), jnp.float32)
    for offset in range(tap_count):
        summed = summed + filter_taps[offset][None, :] * extended[offset : offset + length]
    return summed


def spectral_tables(length):
    doubled = 2 * length
    freqs = lax.broadcasted_iota(jnp.int32, (doubled, length), 0)
    places = lax.broadcasted_iota(jnp.int32, (doubled, length), 1)
    angles = (freqs * places % doubled).astype(jnp.float32) * (2.0 * math.pi / doubled)
    forward = jnp.concatenate([jnp.cos(angles), -jnp.sin(angles)], axis=0)
    inverse = forward.T / doubled
    return (forward, inverse)


def apply_filter(spectrum, signal, forward, inverse):
    middle = forward.shape[0] // 2
    spectra = jnp.dot(forward, signal, precision=HIGHEST)
    real_sig = spectra[:middle]
    imag_sig = spectra[middle:]
    real_filt = spectrum[:middle]
    imag_filt = spectrum[middle:]
    product = jnp.concatenate(
        [real_sig * real_filt - imag_sig * imag_filt, real_sig * imag_filt + imag_sig * real_filt],
        axis=0,
    )
    return jnp.dot(inverse, product, precision=HIGHEST)


def mode_decay(inv_time, length, backward):
    offsets = lax.broadcasted_iota(jnp.float32, (1, length, 1), 1)
    if backward:
        offsets = float(length - 1) - offsets
    return jnp.exp(-offsets * inv_time[:, None, :])


def mode_sums(decay, decay_back, modal_weight, mixed):
    forward_sums = jnp.sum(decay_back * mixed[None], axis=1)
    return (jnp.sum(modal_weight[:, None, :] * decay, axis=0), forward_sums)


def mode_sums_back(decay, grad_long):
    return jnp.sum(decay * grad_long[None], axis=1)


def mode_terms(decay, inv_time, modal_weight, state):
    step_decay = (modal_weight * jnp.exp(-inv_time))[:, None, :]
    term = step_decay * decay * state[:, None, :]
    return jnp.sum(term, axis=0)


def body(
    gate_input,
    key_input,
    value_input,
    short_filters,
    pole_time,
    residues,
    out_weight,
    out_cotangent,
):
    length = gate_input.shape[0]
    tap_count = short_filters.shape[1]
    half = out_weight.shape[1] // 2
    weight_left = lax.all_gather(out_weight[:, :half], "ctx", axis=0, tiled=True)
    weight_right = gather_ctx(out_weight[:, half:]).reshape(-1, half)
    stacked = jnp.stack([gate_input, key_input, value_input])
    tails = from_behind(stacked[:, length - (tap_count - 1) :, :], "ctx", 1)
    extended = jnp.concatenate([tails, stacked], axis=1).astype(jnp.float32)
    gate_short = causal_taps(extended[0], short_filters[0], length)
    key_short = causal_taps(extended[1], short_filters[1], length)
    value_short = causal_taps(extended[2], short_filters[2], length)
    mixed = key_short * value_short
    inv_time = 1.0 / pole_time.T
    modal_weight = residues.T * jnp.sqrt(-jnp.expm1(-2.0 * inv_time))
    block_decay = jnp.exp(-float(length) * inv_time)
    decay = mode_decay(inv_time, length, False)
    decay_back = mode_decay(inv_time, length, True)
    filt_table, forward_sums = mode_sums(decay, decay_back, modal_weight, mixed)
    state_in = carried_in(forward_sums, block_decay, False)
    forward, inverse = spectral_tables(length)
    spectrum = jnp.dot(forward, filt_table, precision=HIGHEST)
    long_local = apply_filter(spectrum, mixed, forward, inverse)
    long_out = long_local + mode_terms(decay, inv_time, modal_weight, state_in)
    gated = (gate_short * long_out).astype(jnp.bfloat16)
    gated_full = lax.all_gather(gated, "chan", axis=1, tiled=True)
    contract = (((1,), (1,)), ((), ()))
    partial = lax.dot_general(
        weight_left, out_cotangent[:, :half], contract, preferred_element_type=jnp.float32
    ) + lax.dot_general(
        weight_right, out_cotangent[:, half:], contract, preferred_element_type=jnp.float32
    )
    partial, _ = lax.optimization_barrier((partial, gated))
    grad_gated = reduce_chan(partial).T
    grad_long = grad_gated * gate_short
    backward_sums = mode_sums_back(decay, grad_long)
    state_back = carried_in(backward_sums, block_decay, True)
    back_local = apply_filter(spectrum, grad_long[::-1], forward, inverse)[::-1]
    grad_mixed = back_local + mode_terms(decay_back, inv_time, modal_weight, state_back)
    grad_gate_short = grad_gated * long_out
    grad_key_short = grad_mixed * value_short
    grad_value_short = grad_mixed * key_short
    grads = jnp.stack([grad_gate_short, grad_key_short, grad_value_short])
    gated_full, grads = lax.optimization_barrier((gated_full, grads))
    block_output = jnp.concatenate(
        [
            jnp.dot(gated_full, weight_left, preferred_element_type=jnp.float32),
            jnp.dot(gated_full, weight_right, preferred_element_type=jnp.float32),
        ],
        axis=1,
    ).astype(jnp.bfloat16)
    heads = from_behind(grads[:, : tap_count - 1, :], "ctx", -1)
    ext_grads = jnp.concatenate([grads, heads], axis=1)
    gate_grad = anti_taps(ext_grads[0], short_filters[0], length).astype(jnp.bfloat16)
    key_grad = anti_taps(ext_grads[1], short_filters[1], length).astype(jnp.bfloat16)
    value_grad = anti_taps(ext_grads[2], short_filters[2], length).astype(jnp.bfloat16)
    return (block_output, gate_grad, key_grad, value_grad)


def solution(mesh):
    in_specs = (
        P("ctx", "chan"),
        P("ctx", "chan"),
        P("ctx", "chan"),
        P(None, None, "chan"),
        P("chan", None),
        P("chan", None),
        P("ctx", "chan"),
        P("ctx", "chan"),
    )
    out_specs = (P("ctx", "chan"), P("ctx", "chan"), P("ctx", "chan"), P("ctx", "chan"))
    return jax.shard_map(body, mesh=mesh, in_specs=in_specs, out_specs=out_specs, check_vma=False)
```

```python
import math

import jax
import jax.numpy as jnp
from jax import lax
from jax.sharding import PartitionSpec as P

HIGHEST = lax.Precision.HIGHEST


def from_behind(block, axis, distance):
    devices = range(lax.axis_size(axis))
    route = [(i - distance, i) for i in devices if i - distance in devices]
    return lax.ppermute(block, axis, route)


def gather_ctx(block):
    peers, position = (lax.axis_size("ctx"), lax.axis_index("ctx"))
    recv = [block] + [
        lax.ppermute(block, "ctx", [(i, (i + d) % peers) for i in range(peers)])
        for d in range(1, peers)
    ]
    order = (position - jnp.arange(peers)) % peers
    return jnp.take(jnp.stack(recv), order, axis=0, mode="clip")


def reduce_chan(weights, cotangents):
    peers, position = (lax.axis_size("chan"), lax.axis_index("chan"))
    contract = (((1,), (1,)), ((), ()))

    def partial_of(bit):
        total = 0.0
        for weight, cot in zip(weights, cotangents):
            rows = weight.reshape(peers // 2, 2, -1, weight.shape[1])
            rows = lax.dynamic_index_in_dim(rows, bit, axis=1, keepdims=False)
            total = total + lax.dot_general(
                rows.reshape(-1, weight.shape[1]), cot, contract, preferred_element_type=jnp.float32
            )
        return total.reshape(peers // 2, -1, total.shape[1])

    give = partial_of(1 - position % 2)
    arrived_half = lax.ppermute(give, "chan", [(j, j ^ 1) for j in range(peers)])
    half = partial_of(position % 2) + arrived_half
    groups = [list(range(b, peers, 2)) for b in range(2)]
    arrived = lax.all_to_all(half, "chan", 0, 0, axis_index_groups=groups, tiled=True)
    return jnp.sum(arrived, axis=0)


def carried_in(sums, block_decay, reverse):
    peers = lax.axis_size("ctx")
    state = jnp.zeros_like(block_decay)
    for d in range(peers - 1, 0, -1):
        route = [(i + d, i) if reverse else (i, i + d) for i in range(peers - d)]
        state = block_decay * state + lax.ppermute(sums, "ctx", route)
    return state


def causal_taps(extended, filter_taps, length):
    tap_count = filter_taps.shape[0]
    summed = jnp.zeros((length, extended.shape[1]), jnp.float32)
    for offset in range(tap_count):
        lead_row = tap_count - 1 - offset
        summed = summed + filter_taps[offset][None, :] * extended[lead_row : lead_row + length]
    return summed


def anti_taps(extended, filter_taps, length):
    tap_count = filter_taps.shape[0]
    summed = jnp.zeros((length, extended.shape[1]), jnp.float32)
    for offset in range(tap_count):
        summed = summed + filter_taps[offset][None, :] * extended[offset : offset + length]
    return summed


def spectral_tables(length):
    doubled = 2 * length
    freqs = lax.broadcasted_iota(jnp.int32, (doubled, length), 0)
    places = lax.broadcasted_iota(jnp.int32, (doubled, length), 1)
    angles = (freqs * places % doubled).astype(jnp.float32) * (2.0 * math.pi / doubled)
    forward = jnp.concatenate([jnp.cos(angles), -jnp.sin(angles)], axis=0)
    inverse = forward.T / doubled
    return (forward, inverse)


def apply_filter(spectrum, signal, forward, inverse):
    middle = forward.shape[0] // 2
    spectra = jnp.dot(forward, signal, precision=HIGHEST)
    real_sig = spectra[:middle]
    imag_sig = spectra[middle:]
    real_filt = spectrum[:middle]
    imag_filt = spectrum[middle:]
    product = jnp.concatenate(
        [real_sig * real_filt - imag_sig * imag_filt, real_sig * imag_filt + imag_sig * real_filt],
        axis=0,
    )
    return jnp.dot(inverse, product, precision=HIGHEST)


def mode_decay(inv_time, length, backward):
    offsets = lax.broadcasted_iota(jnp.float32, (1, length, 1), 1)
    if backward:
        offsets = float(length - 1) - offsets
    return jnp.exp(-offsets * inv_time[:, None, :])


def mode_sums(decay, decay_back, modal_weight, mixed):
    forward_sums = jnp.sum(decay_back * mixed[None], axis=1)
    return (jnp.sum(modal_weight[:, None, :] * decay, axis=0), forward_sums)


def mode_sums_back(decay, grad_long):
    return jnp.sum(decay * grad_long[None], axis=1)


def mode_terms(decay, inv_time, modal_weight, state):
    step_decay = (modal_weight * jnp.exp(-inv_time))[:, None, :]
    term = step_decay * decay * state[:, None, :]
    return jnp.sum(term, axis=0)


def body(
    gate_input,
    key_input,
    value_input,
    short_filters,
    pole_time,
    residues,
    out_weight,
    out_cotangent,
):
    length = gate_input.shape[0]
    tap_count = short_filters.shape[1]
    half = out_weight.shape[1] // 2
    weight_left = lax.all_gather(out_weight[:, :half], "ctx", axis=0, tiled=True)
    weight_right = gather_ctx(out_weight[:, half:]).reshape(-1, half)
    stacked = jnp.stack([gate_input, key_input, value_input])
    tails = from_behind(stacked[:, length - (tap_count - 1) :, :], "ctx", 1)
    extended = jnp.concatenate([tails, stacked], axis=1).astype(jnp.float32)
    gate_short = causal_taps(extended[0], short_filters[0], length)
    key_short = causal_taps(extended[1], short_filters[1], length)
    value_short = causal_taps(extended[2], short_filters[2], length)
    mixed = key_short * value_short
    inv_time = 1.0 / pole_time.T
    modal_weight = residues.T * jnp.sqrt(-jnp.expm1(-2.0 * inv_time))
    block_decay = jnp.exp(-float(length) * inv_time)
    decay = mode_decay(inv_time, length, False)
    decay_back = mode_decay(inv_time, length, True)
    filt_table, forward_sums = mode_sums(decay, decay_back, modal_weight, mixed)
    state_in = carried_in(forward_sums, block_decay, False)
    forward, inverse = spectral_tables(length)
    spectrum = jnp.dot(forward, filt_table, precision=HIGHEST)
    long_local = apply_filter(spectrum, mixed, forward, inverse)
    long_out = long_local + mode_terms(decay, inv_time, modal_weight, state_in)
    gated = (gate_short * long_out).astype(jnp.bfloat16)
    gated_full = lax.all_gather(gated, "chan", axis=1, tiled=True)
    weights, cotangents = lax.optimization_barrier(
        ((weight_left, weight_right), (out_cotangent[:, :half], out_cotangent[:, half:], gated))
    )
    grad_gated = reduce_chan(weights, cotangents[:2]).T
    grad_long = grad_gated * gate_short
    backward_sums = mode_sums_back(decay, grad_long)
    state_back = carried_in(backward_sums, block_decay, True)
    back_local = apply_filter(spectrum, grad_long[::-1], forward, inverse)[::-1]
    grad_mixed = back_local + mode_terms(decay_back, inv_time, modal_weight, state_back)
    grad_gate_short = grad_gated * long_out
    grad_key_short = grad_mixed * value_short
    grad_value_short = grad_mixed * key_short
    grads = jnp.stack([grad_gate_short, grad_key_short, grad_value_short])
    gated_full, grads = lax.optimization_barrier((gated_full, grads))
    block_output = jnp.concatenate(
        [
            jnp.dot(gated_full, weight_left, preferred_element_type=jnp.float32),
            jnp.dot(gated_full, weight_right, preferred_element_type=jnp.float32),
        ],
        axis=1,
    ).astype(jnp.bfloat16)
    heads = from_behind(grads[:, : tap_count - 1, :], "ctx", -1)
    ext_grads = jnp.concatenate([grads, heads], axis=1)
    gate_grad = anti_taps(ext_grads[0], short_filters[0], length).astype(jnp.bfloat16)
    key_grad = anti_taps(ext_grads[1], short_filters[1], length).astype(jnp.bfloat16)
    value_grad = anti_taps(ext_grads[2], short_filters[2], length).astype(jnp.bfloat16)
    return (block_output, gate_grad, key_grad, value_grad)


def solution(mesh):
    in_specs = (
        P("ctx", "chan"),
        P("ctx", "chan"),
        P("ctx", "chan"),
        P(None, None, "chan"),
        P("chan", None),
        P("chan", None),
        P("ctx", "chan"),
        P("ctx", "chan"),
    )
    out_specs = (P("ctx", "chan"), P("ctx", "chan"), P("ctx", "chan"), P("ctx", "chan"))
    return jax.shard_map(body, mesh=mesh, in_specs=in_specs, out_specs=out_specs, check_vma=False)
```

```python
import math

import jax
import jax.numpy as jnp
from jax import lax
from jax.sharding import PartitionSpec as P

HIGHEST = lax.Precision.HIGHEST


def from_behind(block, axis, distance):
    devices = range(lax.axis_size(axis))
    route = [(i - distance, i) for i in devices if i - distance in devices]
    return lax.ppermute(block, axis, route)


def gather_ctx(block):
    peers, position = (lax.axis_size("ctx"), lax.axis_index("ctx"))
    recv = [block] + [
        lax.ppermute(block, "ctx", [(i, (i + d) % peers) for i in range(peers)])
        for d in range(1, peers)
    ]
    order = (position - jnp.arange(peers)) % peers
    return jnp.take(jnp.stack(recv), order, axis=0, mode="clip")


def reduce_chan(weights, cotangents):
    peers, position = (lax.axis_size("chan"), lax.axis_index("chan"))
    contract = (((1,), (1,)), ((), ()))

    def partial_of(bit):
        total = 0.0
        for weight, cot in zip(weights, cotangents):
            rows = weight.reshape(peers // 2, 2, -1, weight.shape[1])
            rows = lax.dynamic_index_in_dim(rows, bit, axis=1, keepdims=False)
            total = total + lax.dot_general(
                rows.reshape(-1, weight.shape[1]), cot, contract, preferred_element_type=jnp.float32
            )
        return total.reshape(peers // 2, -1, total.shape[1])

    give = partial_of(1 - position % 2)
    arrived_half = lax.ppermute(give, "chan", [(j, j ^ 1) for j in range(peers)])
    half = partial_of(position % 2) + arrived_half
    groups = [list(range(b, peers, 2)) for b in range(2)]
    arrived = lax.all_to_all(half, "chan", 0, 0, axis_index_groups=groups, tiled=True)
    return jnp.sum(arrived, axis=0)


def carried_in(sums, block_decay, reverse):
    peers = lax.axis_size("ctx")
    state = jnp.zeros_like(block_decay)
    for d in range(peers - 1, 0, -1):
        route = [(i + d, i) if reverse else (i, i + d) for i in range(peers - d)]
        state = block_decay * state + lax.ppermute(sums, "ctx", route)
    return state


def causal_taps(extended, filter_taps, length):
    tap_count = filter_taps.shape[0]
    summed = jnp.zeros((length, extended.shape[1]), jnp.float32)
    for offset in range(tap_count):
        lead_row = tap_count - 1 - offset
        summed = summed + filter_taps[offset][None, :] * extended[lead_row : lead_row + length]
    return summed


def anti_taps(extended, filter_taps, length):
    tap_count = filter_taps.shape[0]
    summed = jnp.zeros((length, extended.shape[1]), jnp.float32)
    for offset in range(tap_count):
        summed = summed + filter_taps[offset][None, :] * extended[offset : offset + length]
    return summed


def spectral_tables(length):
    doubled = 2 * length
    freqs = lax.broadcasted_iota(jnp.int32, (doubled, length), 0)
    places = lax.broadcasted_iota(jnp.int32, (doubled, length), 1)
    angles = (freqs * places % doubled).astype(jnp.float32) * (2.0 * math.pi / doubled)
    forward = jnp.concatenate([jnp.cos(angles), -jnp.sin(angles)], axis=0)
    inverse = forward.T / doubled
    return (forward, inverse)


def apply_filter(spectrum, signal, forward, inverse):
    middle = forward.shape[0] // 2
    spectra = jnp.dot(forward, signal, precision=HIGHEST)
    real_sig = spectra[:middle]
    imag_sig = spectra[middle:]
    real_filt = spectrum[:middle]
    imag_filt = spectrum[middle:]
    product = jnp.concatenate(
        [real_sig * real_filt - imag_sig * imag_filt, real_sig * imag_filt + imag_sig * real_filt],
        axis=0,
    )
    return jnp.dot(inverse, product, precision=HIGHEST)


def mode_decay(inv_time, length, backward):
    offsets = lax.broadcasted_iota(jnp.float32, (1, length, 1), 1)
    if backward:
        offsets = float(length - 1) - offsets
    return jnp.exp(-offsets * inv_time[:, None, :])


def mode_sums(decay, decay_back, modal_weight, mixed):
    forward_sums = jnp.sum(decay_back * mixed[None], axis=1)
    return (jnp.sum(modal_weight[:, None, :] * decay, axis=0), forward_sums)


def mode_sums_back(decay, grad_long):
    return jnp.sum(decay * grad_long[None], axis=1)


def mode_terms(decay, inv_time, modal_weight, state):
    step_decay = (modal_weight * jnp.exp(-inv_time))[:, None, :]
    term = step_decay * decay * state[:, None, :]
    return jnp.sum(term, axis=0)


def body(
    gate_input,
    key_input,
    value_input,
    short_filters,
    pole_time,
    residues,
    out_weight,
    out_cotangent,
):
    length = gate_input.shape[0]
    tap_count = short_filters.shape[1]
    half = out_weight.shape[1] // 2
    rows = out_weight.shape[0] * 3 // 4
    left = out_weight[:, :half]
    weight_left = jnp.concatenate(
        [lax.all_gather(left[:rows], "ctx", axis=0), gather_ctx(left[rows:])], axis=1
    ).reshape(-1, half)
    weight_right = gather_ctx(out_weight[:, half:]).reshape(-1, half)
    stacked = jnp.stack([gate_input, key_input, value_input])
    tails = from_behind(stacked[:, length - (tap_count - 1) :, :], "ctx", 1)
    extended = jnp.concatenate([tails, stacked], axis=1).astype(jnp.float32)
    gate_short = causal_taps(extended[0], short_filters[0], length)
    key_short = causal_taps(extended[1], short_filters[1], length)
    value_short = causal_taps(extended[2], short_filters[2], length)
    mixed = key_short * value_short
    inv_time = 1.0 / pole_time.T
    modal_weight = residues.T * jnp.sqrt(-jnp.expm1(-2.0 * inv_time))
    block_decay = jnp.exp(-float(length) * inv_time)
    decay = mode_decay(inv_time, length, False)
    decay_back = mode_decay(inv_time, length, True)
    filt_table, forward_sums = mode_sums(decay, decay_back, modal_weight, mixed)
    state_in = carried_in(forward_sums, block_decay, False)
    forward, inverse = spectral_tables(length)
    spectrum = jnp.dot(forward, filt_table, precision=HIGHEST)
    long_local = apply_filter(spectrum, mixed, forward, inverse)
    long_out = long_local + mode_terms(decay, inv_time, modal_weight, state_in)
    gated = (gate_short * long_out).astype(jnp.bfloat16)
    gated_full = lax.all_gather(gated, "chan", axis=1, tiled=True)
    weights, cotangents = lax.optimization_barrier(
        ((weight_left, weight_right), (out_cotangent[:, :half], out_cotangent[:, half:], gated))
    )
    grad_gated = reduce_chan(weights, cotangents[:2]).T
    grad_long = grad_gated * gate_short
    backward_sums = mode_sums_back(decay, grad_long)
    state_back = carried_in(backward_sums, block_decay, True)
    back_local = apply_filter(spectrum, grad_long[::-1], forward, inverse)[::-1]
    grad_mixed = back_local + mode_terms(decay_back, inv_time, modal_weight, state_back)
    grad_gate_short = grad_gated * long_out
    grad_key_short = grad_mixed * value_short
    grad_value_short = grad_mixed * key_short
    grads = jnp.stack([grad_gate_short, grad_key_short, grad_value_short])
    gated_full, grads = lax.optimization_barrier((gated_full, grads))
    block_output = jnp.concatenate(
        [
            jnp.dot(gated_full, weight_left, preferred_element_type=jnp.float32),
            jnp.dot(gated_full, weight_right, preferred_element_type=jnp.float32),
        ],
        axis=1,
    ).astype(jnp.bfloat16)
    heads = from_behind(grads[:, : tap_count - 1, :], "ctx", -1)
    ext_grads = jnp.concatenate([grads, heads], axis=1)
    gate_grad = anti_taps(ext_grads[0], short_filters[0], length).astype(jnp.bfloat16)
    key_grad = anti_taps(ext_grads[1], short_filters[1], length).astype(jnp.bfloat16)
    value_grad = anti_taps(ext_grads[2], short_filters[2], length).astype(jnp.bfloat16)
    return (block_output, gate_grad, key_grad, value_grad)


def solution(mesh):
    in_specs = (
        P("ctx", "chan"),
        P("ctx", "chan"),
        P("ctx", "chan"),
        P(None, None, "chan"),
        P("chan", None),
        P("chan", None),
        P("ctx", "chan"),
        P("ctx", "chan"),
    )
    out_specs = (P("ctx", "chan"), P("ctx", "chan"), P("ctx", "chan"), P("ctx", "chan"))
    return jax.shard_map(body, mesh=mesh, in_specs=in_specs, out_specs=out_specs, check_vma=False)
```

```python
import math

import jax
import jax.numpy as jnp
from jax import lax
from jax.sharding import PartitionSpec as P

HIGHEST = lax.Precision.HIGHEST


def from_behind(block, axis, distance):
    devices = range(lax.axis_size(axis))
    route = [(i - distance, i) for i in devices if i - distance in devices]
    return lax.ppermute(block, axis, route)


def gather_ctx(block):
    peers, position = (lax.axis_size("ctx"), lax.axis_index("ctx"))
    recv = [block] + [
        lax.ppermute(block, "ctx", [(i, (i + d) % peers) for i in range(peers)])
        for d in range(1, peers)
    ]
    order = (position - jnp.arange(peers)) % peers
    return jnp.take(jnp.stack(recv), order, axis=0, mode="clip")


def reduce_chan(weights, cotangents):
    peers, position = (lax.axis_size("chan"), lax.axis_index("chan"))
    contract = (((1,), (1,)), ((), ()))

    def partial_of(bit):
        total = 0.0
        for weight, cot in zip(weights, cotangents):
            rows = weight.reshape(peers // 2, 2, -1, weight.shape[1])
            rows = lax.dynamic_index_in_dim(rows, bit, axis=1, keepdims=False)
            total = total + lax.dot_general(
                rows.reshape(-1, weight.shape[1]), cot, contract, preferred_element_type=jnp.float32
            )
        return total.reshape(peers // 2, -1, total.shape[1])

    give = partial_of(1 - position % 2)
    arrived_half = lax.ppermute(give, "chan", [(j, j ^ 1) for j in range(peers)])
    half = partial_of(position % 2) + arrived_half
    groups = [list(range(b, peers, 2)) for b in range(2)]
    arrived = lax.all_to_all(half, "chan", 0, 0, axis_index_groups=groups, tiled=True)
    return jnp.sum(arrived, axis=0)


def carried_in(sums, block_decay, reverse):
    peers = lax.axis_size("ctx")
    state = jnp.zeros_like(block_decay)
    for d in range(peers - 1, 0, -1):
        route = [(i + d, i) if reverse else (i, i + d) for i in range(peers - d)]
        state = block_decay * state + lax.ppermute(sums, "ctx", route)
    return state


def causal_taps(extended, filter_taps, length):
    tap_count = filter_taps.shape[0]
    summed = jnp.zeros((length, extended.shape[1]), jnp.float32)
    for offset in range(tap_count):
        lead_row = tap_count - 1 - offset
        summed = summed + filter_taps[offset][None, :] * extended[lead_row : lead_row + length]
    return summed


def anti_taps(extended, filter_taps, length):
    tap_count = filter_taps.shape[0]
    summed = jnp.zeros((length, extended.shape[1]), jnp.float32)
    for offset in range(tap_count):
        summed = summed + filter_taps[offset][None, :] * extended[offset : offset + length]
    return summed


def spectral_tables(length):
    doubled = 2 * length
    freqs = lax.broadcasted_iota(jnp.int32, (doubled, length), 0)
    places = lax.broadcasted_iota(jnp.int32, (doubled, length), 1)
    angles = (freqs * places % doubled).astype(jnp.float32) * (2.0 * math.pi / doubled)
    forward = jnp.concatenate([jnp.cos(angles), -jnp.sin(angles)], axis=0)
    inverse = forward.T / doubled
    return (forward, inverse)


def apply_filter(spectrum, signal, forward, inverse):
    middle = forward.shape[0] // 2
    spectra = jnp.dot(forward, signal, precision=HIGHEST)
    real_sig = spectra[:middle]
    imag_sig = spectra[middle:]
    real_filt = spectrum[:middle]
    imag_filt = spectrum[middle:]
    product = jnp.concatenate(
        [real_sig * real_filt - imag_sig * imag_filt, real_sig * imag_filt + imag_sig * real_filt],
        axis=0,
    )
    return jnp.dot(inverse, product, precision=HIGHEST)


def mode_decay(inv_time, length, backward):
    offsets = lax.broadcasted_iota(jnp.float32, (1, length, 1), 1)
    if backward:
        offsets = float(length - 1) - offsets
    return jnp.exp(-offsets * inv_time[:, None, :])


def mode_sums(decay, decay_back, modal_weight, mixed):
    forward_sums = jnp.sum(decay_back * mixed[None], axis=1)
    return (jnp.sum(modal_weight[:, None, :] * decay, axis=0), forward_sums)


def mode_sums_back(decay, grad_long):
    return jnp.sum(decay * grad_long[None], axis=1)


def mode_terms(decay, inv_time, modal_weight, state):
    step_decay = (modal_weight * jnp.exp(-inv_time))[:, None, :]
    term = step_decay * decay * state[:, None, :]
    return jnp.sum(term, axis=0)


def body(
    gate_input,
    key_input,
    value_input,
    short_filters,
    pole_time,
    residues,
    out_weight,
    out_cotangent,
):
    length = gate_input.shape[0]
    tap_count = short_filters.shape[1]
    half = out_weight.shape[1] // 2
    weight_left = lax.all_gather(out_weight[:, :half], "ctx", axis=0, tiled=True)
    weight_right = gather_ctx(out_weight[:, half:]).reshape(-1, half)
    stacked = jnp.stack([gate_input, key_input, value_input])
    tails = from_behind(stacked[:, length - (tap_count - 1) :, :], "ctx", 1)
    extended = jnp.concatenate([tails, stacked], axis=1).astype(jnp.float32)
    gate_short = causal_taps(extended[0], short_filters[0], length)
    key_short = causal_taps(extended[1], short_filters[1], length)
    value_short = causal_taps(extended[2], short_filters[2], length)
    mixed = key_short * value_short
    inv_time = 1.0 / pole_time.T
    modal_weight = residues.T * jnp.sqrt(-jnp.expm1(-2.0 * inv_time))
    block_decay = jnp.exp(-float(length) * inv_time)
    decay = mode_decay(inv_time, length, False)
    decay_back = mode_decay(inv_time, length, True)
    filt_table, forward_sums = mode_sums(decay, decay_back, modal_weight, mixed)
    state_in = carried_in(forward_sums, block_decay, False)
    forward, inverse = spectral_tables(length)
    spectrum = jnp.dot(forward, filt_table, precision=HIGHEST)
    long_local = apply_filter(spectrum, mixed, forward, inverse)
    long_out = long_local + mode_terms(decay, inv_time, modal_weight, state_in)
    gated = (gate_short * long_out).astype(jnp.bfloat16)
    gated_full = lax.all_gather(gated, "chan", axis=1, tiled=True)
    weights, cotangents = lax.optimization_barrier(
        ((weight_left, weight_right), (out_cotangent[:, :half], out_cotangent[:, half:], gated))
    )
    grad_gated = reduce_chan(weights, cotangents[:2]).T
    grad_long = grad_gated * gate_short
    backward_sums = mode_sums_back(decay, grad_long)
    state_back = carried_in(backward_sums, block_decay, True)
    back_local = apply_filter(spectrum, grad_long[::-1], forward, inverse)[::-1]
    grad_mixed = back_local + mode_terms(decay_back, inv_time, modal_weight, state_back)
    grad_gate_short = grad_gated * long_out
    grad_key_short = grad_mixed * value_short
    grad_value_short = grad_mixed * key_short
    grads = jnp.stack([grad_gate_short, grad_key_short, grad_value_short])
    gated_full, _ = lax.optimization_barrier((gated_full, grads))
    block_output = jnp.concatenate(
        [
            jnp.dot(gated_full, weight_left, preferred_element_type=jnp.float32),
            jnp.dot(gated_full, weight_right, preferred_element_type=jnp.float32),
        ],
        axis=1,
    ).astype(jnp.bfloat16)
    heads = from_behind(grads[:, : tap_count - 1, :], "ctx", -1)
    ext_grads = jnp.concatenate([grads, heads], axis=1)
    gate_grad = anti_taps(ext_grads[0], short_filters[0], length).astype(jnp.bfloat16)
    key_grad = anti_taps(ext_grads[1], short_filters[1], length).astype(jnp.bfloat16)
    value_grad = anti_taps(ext_grads[2], short_filters[2], length).astype(jnp.bfloat16)
    return (block_output, gate_grad, key_grad, value_grad)


def solution(mesh):
    in_specs = (
        P("ctx", "chan"),
        P("ctx", "chan"),
        P("ctx", "chan"),
        P(None, None, "chan"),
        P("chan", None),
        P("chan", None),
        P("ctx", "chan"),
        P("ctx", "chan"),
    )
    out_specs = (P("ctx", "chan"), P("ctx", "chan"), P("ctx", "chan"), P("ctx", "chan"))
    return jax.shard_map(body, mesh=mesh, in_specs=in_specs, out_specs=out_specs, check_vma=False)
```

```python
import math

import jax
import jax.numpy as jnp
from jax import lax
from jax.sharding import PartitionSpec as P

HIGHEST = lax.Precision.HIGHEST


def from_behind(block, axis, distance):
    devices = range(lax.axis_size(axis))
    route = [(i - distance, i) for i in devices if i - distance in devices]
    return lax.ppermute(block, axis, route)


def gather_ctx(block):
    peers, position = (lax.axis_size("ctx"), lax.axis_index("ctx"))
    recv = [block] + [
        lax.ppermute(block, "ctx", [(i, (i + d) % peers) for i in range(peers)])
        for d in range(1, peers)
    ]
    order = (position - jnp.arange(peers)) % peers
    return jnp.take(jnp.stack(recv), order, axis=0, mode="clip")


def reduce_chan(weights, cotangents):
    peers, position = (lax.axis_size("chan"), lax.axis_index("chan"))
    contract = (((1,), (1,)), ((), ()))

    def partial_of(bit):
        total = 0.0
        for weight, cot in zip(weights, cotangents):
            rows = weight.reshape(peers // 2, 2, -1, weight.shape[1])
            rows = lax.dynamic_index_in_dim(rows, bit, axis=1, keepdims=False)
            total = total + lax.dot_general(
                rows.reshape(-1, weight.shape[1]), cot, contract, preferred_element_type=jnp.float32
            )
        return total.reshape(peers // 2, -1, total.shape[1])

    give = partial_of(1 - position % 2)
    arrived_half = lax.ppermute(give, "chan", [(j, j ^ 1) for j in range(peers)])
    half = partial_of(position % 2) + arrived_half
    groups = [list(range(b, peers, 2)) for b in range(2)]
    arrived = lax.all_to_all(half, "chan", 0, 0, axis_index_groups=groups, tiled=True)
    return jnp.sum(arrived, axis=0)


def carried_in(sums, block_decay, reverse):
    peers = lax.axis_size("ctx")
    state = jnp.zeros_like(block_decay)
    for d in range(peers - 1, 0, -1):
        route = [(i + d, i) if reverse else (i, i + d) for i in range(peers - d)]
        state = block_decay * state + lax.ppermute(sums, "ctx", route)
    return state


def causal_taps(extended, filter_taps, length):
    tap_count = filter_taps.shape[0]
    summed = jnp.zeros((length, extended.shape[1]), jnp.float32)
    for offset in range(tap_count):
        lead_row = tap_count - 1 - offset
        summed = summed + filter_taps[offset][None, :] * extended[lead_row : lead_row + length]
    return summed


def anti_taps(extended, filter_taps, length):
    tap_count = filter_taps.shape[0]
    summed = jnp.zeros((length, extended.shape[1]), jnp.float32)
    for offset in range(tap_count):
        summed = summed + filter_taps[offset][None, :] * extended[offset : offset + length]
    return summed


def spectral_tables(length):
    doubled = 2 * length
    freqs = lax.broadcasted_iota(jnp.int32, (doubled, length), 0)
    places = lax.broadcasted_iota(jnp.int32, (doubled, length), 1)
    angles = (freqs * places % doubled).astype(jnp.float32) * (2.0 * math.pi / doubled)
    forward = jnp.concatenate([jnp.cos(angles), -jnp.sin(angles)], axis=0)
    inverse = forward.T / doubled
    return (forward, inverse)


def apply_filter(spectrum, signal, forward, inverse):
    middle = forward.shape[0] // 2
    spectra = jnp.dot(forward, signal, precision=HIGHEST)
    real_sig = spectra[:middle]
    imag_sig = spectra[middle:]
    real_filt = spectrum[:middle]
    imag_filt = spectrum[middle:]
    product = jnp.concatenate(
        [real_sig * real_filt - imag_sig * imag_filt, real_sig * imag_filt + imag_sig * real_filt],
        axis=0,
    )
    return jnp.dot(inverse, product, precision=HIGHEST)


def mode_decay(inv_time, length, backward):
    offsets = lax.broadcasted_iota(jnp.float32, (1, length, 1), 1)
    if backward:
        offsets = float(length - 1) - offsets
    return jnp.exp(-offsets * inv_time[:, None, :])


def mode_sums(decay, decay_back, modal_weight, mixed):
    forward_sums = jnp.sum(decay_back * mixed[None], axis=1)
    return (jnp.sum(modal_weight[:, None, :] * decay, axis=0), forward_sums)


def mode_sums_back(decay, grad_long):
    return jnp.sum(decay * grad_long[None], axis=1)


def mode_terms(decay, inv_time, modal_weight, state):
    step_decay = (modal_weight * jnp.exp(-inv_time))[:, None, :]
    term = step_decay * decay * state[:, None, :]
    return jnp.sum(term, axis=0)


def body(
    gate_input,
    key_input,
    value_input,
    short_filters,
    pole_time,
    residues,
    out_weight,
    out_cotangent,
):
    length = gate_input.shape[0]
    tap_count = short_filters.shape[1]
    half = out_weight.shape[1] // 2
    left = out_weight[:, :half]
    weight_left = lax.all_to_all(
        jnp.broadcast_to(left[None], (lax.axis_size("ctx"),) + left.shape), "ctx", 0, 0, tiled=True
    ).reshape(-1, half)
    weight_right = gather_ctx(out_weight[:, half:]).reshape(-1, half)
    stacked = jnp.stack([gate_input, key_input, value_input])
    tails = from_behind(stacked[:, length - (tap_count - 1) :, :], "ctx", 1)
    extended = jnp.concatenate([tails, stacked], axis=1).astype(jnp.float32)
    gate_short = causal_taps(extended[0], short_filters[0], length)
    key_short = causal_taps(extended[1], short_filters[1], length)
    value_short = causal_taps(extended[2], short_filters[2], length)
    mixed = key_short * value_short
    inv_time = 1.0 / pole_time.T
    modal_weight = residues.T * jnp.sqrt(-jnp.expm1(-2.0 * inv_time))
    block_decay = jnp.exp(-float(length) * inv_time)
    decay = mode_decay(inv_time, length, False)
    decay_back = mode_decay(inv_time, length, True)
    filt_table, forward_sums = mode_sums(decay, decay_back, modal_weight, mixed)
    state_in = carried_in(forward_sums, block_decay, False)
    forward, inverse = spectral_tables(length)
    spectrum = jnp.dot(forward, filt_table, precision=HIGHEST)
    long_local = apply_filter(spectrum, mixed, forward, inverse)
    long_out = long_local + mode_terms(decay, inv_time, modal_weight, state_in)
    gated = (gate_short * long_out).astype(jnp.bfloat16)
    gated_full = lax.all_gather(gated, "chan", axis=1, tiled=True)
    weights, cotangents = lax.optimization_barrier(
        ((weight_left, weight_right), (out_cotangent[:, :half], out_cotangent[:, half:], gated))
    )
    grad_gated = reduce_chan(weights, cotangents[:2]).T
    grad_long = grad_gated * gate_short
    backward_sums = mode_sums_back(decay, grad_long)
    state_back = carried_in(backward_sums, block_decay, True)
    back_local = apply_filter(spectrum, grad_long[::-1], forward, inverse)[::-1]
    grad_mixed = back_local + mode_terms(decay_back, inv_time, modal_weight, state_back)
    grad_gate_short = grad_gated * long_out
    grad_key_short = grad_mixed * value_short
    grad_value_short = grad_mixed * key_short
    grads = jnp.stack([grad_gate_short, grad_key_short, grad_value_short])
    gated_full, grads = lax.optimization_barrier((gated_full, grads))
    block_output = jnp.concatenate(
        [
            jnp.dot(gated_full, weight_left, preferred_element_type=jnp.float32),
            jnp.dot(gated_full, weight_right, preferred_element_type=jnp.float32),
        ],
        axis=1,
    ).astype(jnp.bfloat16)
    heads = from_behind(grads[:, : tap_count - 1, :], "ctx", -1)
    ext_grads = jnp.concatenate([grads, heads], axis=1)
    gate_grad = anti_taps(ext_grads[0], short_filters[0], length).astype(jnp.bfloat16)
    key_grad = anti_taps(ext_grads[1], short_filters[1], length).astype(jnp.bfloat16)
    value_grad = anti_taps(ext_grads[2], short_filters[2], length).astype(jnp.bfloat16)
    return (block_output, gate_grad, key_grad, value_grad)


def solution(mesh):
    in_specs = (
        P("ctx", "chan"),
        P("ctx", "chan"),
        P("ctx", "chan"),
        P(None, None, "chan"),
        P("chan", None),
        P("chan", None),
        P("ctx", "chan"),
        P("ctx", "chan"),
    )
    out_specs = (P("ctx", "chan"), P("ctx", "chan"), P("ctx", "chan"), P("ctx", "chan"))
    return jax.shard_map(body, mesh=mesh, in_specs=in_specs, out_specs=out_specs, check_vma=False)
```
